32 devices in a mesh: dp: 16 (over z, x, core), tensor: 2 (over y).
Axes of the slice: x: 2, y: 2, z: 4, core: 2. Of those that a mesh axis runs over, the one named last changes fastest.
Arguments:
- context: bfloat16 [4096, 4096], P('dp', 'tensor'), may hold values from -6 to 6
- w_out: bfloat16 [4096, 4096], P('tensor'), may hold values from -1 to 1
- teacher_input: bfloat16 [4096, 4096], P(('dp', 'tensor')), may hold values from -6 to 6
- teacher_gain: bfloat16 [4096], replicated, may hold values from 0.5 to 1.5
- layer_weights: float32 [2], replicated, may hold values from 0.3 to 1.5
- teacher_head: bfloat16 [4096, 4], replicated, may hold values from -16 to 16
- student_hidden: bfloat16 [4096, 3072], P(('dp', 'tensor')), may hold values from -6 to 6
- student_input: bfloat16 [4096, 768], P(('dp', 'tensor')), may hold values from -10 to 10
- down_weight: bfloat16 [3072, 768], P(('dp', 'tensor')), may hold values from -0.109375 to 0.109375
- student_gain: bfloat16 [768], replicated, may hold values from 0.5 to 1.5
- student_head: bfloat16 [768, 4], replicated, may hold values from -32 to 32
- labels: int32 [4096], P(('dp', 'tensor')), may hold values from 0 to 3
- lengths: int32 [8], replicated, may hold values from 64 to 512
Outputs:
- grad_down: float32 [3072, 768], P(('dp', 'tensor'))
- grad_head: float32 [768, 4], replicated
- loss: float32 [], replicated
The draws below stay inside these ranges and needn't reach their ends.
All inputs are finite; a program needn't handle non-finite values.
Results may differ from the reference program's by a relative error of at most 0.0075.
Values may be sent and summed in bfloat16 or wider, within the bound.
No kernel may reach another device: no remote copies, remote signals or barrier semaphores. Data moves between devices by JAX's collectives and lax.ppermute only.
A program may use at most 128 MiB of HBM per device.

```python
import math
import jax
import jax.numpy as jnp
from jax import lax

DT = 4096
D = 768
FF = 3072
CLASSES = 4
TOK_DEV = 128
SEQ = 512
TOKENS = 4096
SENTS = 8
N_DP = 16
N_TENSOR = 2


def signs_of(key, shape):
    return jnp.where(jax.random.bernoulli(key, 0.5, shape), 1.0, -1.0).astype(jnp.float32)


def shared_parts(key):
    in_dir = signs_of(jax.random.fold_in(key, 11), (DT,))
    out_dir = signs_of(jax.random.fold_in(key, 12), (DT,))
    token_sign = signs_of(jax.random.fold_in(key, 13), (TOKENS,))
    token_size = jax.random.uniform(jax.random.fold_in(key, 14), (TOKENS,), jnp.float32, 0.7, 1.3)
    return (in_dir, out_dir, token_sign * token_size)


def rough_noise(key, shape):
    return jnp.clip(jax.random.normal(key, shape, jnp.float32), -4.0, 4.0)


def draw_context(key, part):
    in_dir, out_dir, token_share = shared_parts(key)
    noise = rough_noise(jax.random.fold_in(key, 21), (TOKENS, DT))
    return (noise + token_share[:, None] * in_dir[None, :]).astype(jnp.bfloat16)


def draw_teacher_input(key, part):
    in_dir, out_dir, token_share = shared_parts(key)
    noise = rough_noise(jax.random.fold_in(key, 31), (TOKENS, DT))
    return (noise + token_share[:, None] * out_dir[None, :]).astype(jnp.bfloat16)


def draw_w_out(key, part):
    in_dir, out_dir, token_share = shared_parts(key)
    noise = rough_noise(jax.random.fold_in(key, 41), (DT, DT)) * (1.0 / math.sqrt(DT))
    aligned = in_dir[:, None] * out_dir[None, :] * (3.0 / DT)
    return (noise + aligned).astype(jnp.bfloat16)


def draw_student_input(key, part):
    return jnp.clip(jax.random.normal(jax.random.fold_in(key, 51), (TOKENS, D), jnp.float32), -6.0, 6.0).astype(jnp.bfloat16)


def draw_teacher_head(key, part):
    first = jax.random.fold_in(key, 0)
    basis = jnp.clip(jax.random.normal(first, (DT, CLASSES), jnp.float32), -3.0, 3.0)
    return (basis * (2.0 / math.sqrt(DT))).astype(jnp.bfloat16)


def draw_student_head(key, part):
    first = jax.random.fold_in(key, 0)
    basis = jnp.clip(jax.random.normal(first, (D, CLASSES), jnp.float32), -3.0, 3.0)
    return (basis * (2.0 / math.sqrt(D))).astype(jnp.bfloat16)


def with_ends(values, stream_key, smallest, high):
    extent = values.shape
    spot = [jax.random.randint(jax.random.fold_in(stream_key, axis), (), 0, extent[axis]) for axis in range(len(extent))]
    values = values.at[tuple(spot)].set(smallest)
    longest = extent.index(max(extent))
    spot[longest] = (spot[longest] + 1) % extent[longest]
    return values.at[tuple(spot)].set(high)


def strengthened(values, stream_key, source, target, blocks, factor):
    def block_of(axis_at):
        return (jnp.arange(values.shape[axis_at]) // (values.shape[axis_at] // blocks)).reshape((-1,) + (1,) * (values.ndim - 1 - axis_at))

    near = jax.random.permutation(stream_key, blocks)[block_of(target)]
    other_side = (block_of(target) + blocks // 2) % blocks
    return jnp.where((block_of(source) == near) | (block_of(source) == other_side), factor * values, values)


def block_levels(key, extent, cuts, low, largest):
    def one(dim, parts):
        steps = jax.random.uniform(jax.random.fold_in(jax.random.fold_in(key, 6), dim), (parts,), jnp.float32, low / len(cuts), largest / len(cuts))
        return jnp.repeat(jnp.exp(steps), extent[dim] // parts).reshape((-1,) + (1,) * (len(extent) - dim - 1))

    factor_of = one(*cuts[0])
    for cut in cuts[1:]:
        factor_of = factor_of * one(*cut)
    return factor_of


def bell_draw(rng, dims, deviation, most, cuts=(), kind=jnp.bfloat16):
    level = block_levels(rng, dims, cuts, -0.22, 0.18) if cuts else 1.0
    values = jax.random.normal(rng, dims, jnp.float32) * deviation * level
    return jnp.minimum(jnp.maximum(values, -most), most).astype(kind)


def gaussian_with(rng, extent, scale, bound, cuts, heavy, held_as=jnp.bfloat16):
    drawn = scale * jax.random.normal(rng, extent, jnp.float32)
    if cuts:
        drawn = drawn * block_levels(rng, extent, cuts, -0.22, 0.18)
    return jnp.clip(strengthened(drawn, jax.random.fold_in(rng, 3), *heavy), -bound, bound).astype(held_as)


def setup_inputs(seed: int = 0) -> dict:
    arg_keys = jax.random.split(jax.random.key(seed), 14)
    return {
        "context": draw_context(jax.random.fold_in(arg_keys[13], 71), 0),
        "w_out": draw_w_out(jax.random.fold_in(arg_keys[13], 71), 0),
        "teacher_input": draw_teacher_input(jax.random.fold_in(arg_keys[13], 71), 0),
        "teacher_gain": jnp.clip(1.0 + 0.1 * jax.random.normal(arg_keys[3], (DT,), jnp.float32), 0.5, 1.5).astype(jnp.bfloat16),
        "layer_weights": jnp.clip(jnp.exp(jax.random.uniform(arg_keys[4], (2,), jnp.float32, math.log(0.3), math.log(1.5))), 0.3, 1.5),
        "teacher_head": draw_teacher_head(jax.random.fold_in(arg_keys[13], 71), 0),
        "student_hidden": gaussian_with(arg_keys[6], (TOKENS, FF), 1.0, 6.0, ((0, 32),), (0, 1, 32, 2.75)),
        "student_input": draw_student_input(jax.random.fold_in(arg_keys[13], 71), 0),
        "down_weight": bell_draw(arg_keys[8], (FF, D), FF ** -0.5, 0.109375, ((0, 32),)),
        "student_gain": jnp.clip(1.0 + 0.1 * jax.random.normal(arg_keys[9], (D,), jnp.float32), 0.5, 1.5).astype(jnp.bfloat16),
        "student_head": draw_student_head(jax.random.fold_in(arg_keys[13], 71), 0),
        "labels": with_ends(jax.random.randint(arg_keys[11], (TOKENS,), 0, CLASSES), jax.random.fold_in(arg_keys[11], 1), 0, CLASSES - 1).astype(jnp.int32),
        "lengths": with_ends(jax.random.randint(arg_keys[12], (SENTS,), SEQ // 8, SEQ + 1), jax.random.fold_in(arg_keys[12], 1), SEQ // 8, SEQ).astype(jnp.int32),
    }


label_weight = 0.5
teacher_eps = 1e-05
student_eps = 1e-07

def norm_rows(values, gain_vec, epsilon):
    center = values - lax.optimization_barrier(jnp.mean(values, axis=-1, keepdims=True))
    spread = lax.optimization_barrier(jnp.mean(center * center, axis=-1, keepdims=True))
    inverse = lax.rsqrt(spread + epsilon)
    scaled = center * inverse
    return (scaled * gain_vec, scaled, inverse)

def reference(context, w_out, teacher_input, teacher_gain, layer_weights, teacher_head, student_hidden, student_input, down_weight, student_gain, student_head, labels, lengths):
    group_rows = TOK_DEV * N_TENSOR
    shard_cols = DT // N_TENSOR
    positions = jnp.arange(TOKENS, dtype=jnp.int32)
    lengths_tok = lengths[positions // SEQ]
    validity = (positions % SEQ < lengths_tok).astype(jnp.float32)
    sliced = (context.reshape(N_DP, group_rows, DT), teacher_input.reshape(N_DP, group_rows, DT), student_hidden.reshape(N_DP, group_rows, FF), student_input.reshape(N_DP, group_rows, D), labels.reshape(N_DP, group_rows), validity.reshape(N_DP, group_rows))
    teacher_scale = teacher_gain.astype(jnp.float32)
    student_scale = student_gain.astype(jnp.float32)
    classes_row = jnp.arange(CLASSES, dtype=jnp.int32)

    def advance(running, inputs):
        down_sum, head_sum, loss_sum, count_sum = running
        context_rows, teacher_rows, hidden_rows, student_rows, label_rows, valid_rows = inputs
        attention = jnp.zeros((group_rows, DT), jnp.float32)
        for member in range(N_TENSOR):
            partial_value = jnp.dot(context_rows[:, member * shard_cols:(member + 1) * shard_cols], w_out[member * shard_cols:(member + 1) * shard_cols], preferred_element_type=jnp.float32)
            partial_value = lax.optimization_barrier(partial_value.astype(jnp.bfloat16))
            attention = attention + partial_value.astype(jnp.float32)
        residual = teacher_rows.astype(jnp.float32)
        layer_out = norm_rows(residual + attention, teacher_scale, teacher_eps)[0]
        blended = (layer_weights[0] * residual + layer_weights[1] * layer_out).astype(jnp.bfloat16)
        teacher_logits = jnp.dot(blended, teacher_head, preferred_element_type=jnp.float32)
        teacher_logp = jax.nn.log_softmax(teacher_logits, axis=-1)
        teacher_prob = jnp.exp(teacher_logp)
        ffn_out = jnp.dot(hidden_rows, down_weight, preferred_element_type=jnp.float32)
        normed, scaled, inverse = norm_rows(student_rows.astype(jnp.float32) + ffn_out, student_scale, student_eps)
        features = normed.astype(jnp.bfloat16)
        student_logits = jnp.dot(features, student_head, preferred_element_type=jnp.float32)
        student_logp = jax.nn.log_softmax(student_logits, axis=-1)
        student_prob = jnp.exp(student_logp)
        onehot = (label_rows[:, None] == classes_row[None, :]).astype(jnp.float32)
        token_loss = lax.optimization_barrier(jnp.sum(teacher_prob * (teacher_logp - student_logp), axis=1)) - label_weight * lax.optimization_barrier(jnp.sum(onehot * student_logp, axis=1))
        logit_grad = (valid_rows[:, None] * ((1.0 + label_weight) * student_prob - teacher_prob - label_weight * onehot)).astype(jnp.bfloat16)
        head_term = lax.dot_general(features, logit_grad, (((0,), (0,)), ((), ())), preferred_element_type=jnp.float32)
        norm_grad = jnp.dot(logit_grad, student_head.T, preferred_element_type=jnp.float32) * student_scale
        grad_out = ((norm_grad - lax.optimization_barrier(jnp.mean(norm_grad, axis=-1, keepdims=True)) - scaled * lax.optimization_barrier(jnp.mean(norm_grad * scaled, axis=-1, keepdims=True))) * inverse).astype(jnp.bfloat16)
        down_term = lax.dot_general(hidden_rows, grad_out, (((0,), (0,)), ((), ())), preferred_element_type=jnp.float32)
        return ((down_sum + down_term, head_sum + head_term, loss_sum + jnp.sum(valid_rows * token_loss), count_sum + jnp.sum(valid_rows)), None)
    start_state = (jnp.zeros((FF, D), jnp.float32), jnp.zeros((D, CLASSES), jnp.float32), jnp.zeros((), jnp.float32), jnp.zeros((), jnp.float32))
    final_state, unused = lax.scan(advance, start_state, sliced)
    down_sum, head_sum, loss_sum, count_sum = final_state
    return (down_sum, head_sum, loss_sum / count_sum)
```

```python
import jax
import jax.numpy as jnp
import numpy as np
from jax import lax
from jax.sharding import Mesh
from jax.sharding import PartitionSpec as P

SEQ = 512


label_weight = 0.5
teacher_eps = 1e-05
student_eps = 1e-07

TOKS = ("g", "c", "tensor")


def norm_rows(values, gain_vec, epsilon):
    center = values - jnp.mean(values, axis=-1, keepdims=True)
    spread = jnp.mean(center * center, axis=-1, keepdims=True)
    inverse = lax.rsqrt(spread + epsilon)
    scaled = center * inverse
    return (scaled * gain_vec, scaled, inverse)


def folder(ordered, row_piece):
    return jnp.dot(ordered, row_piece, preferred_element_type=jnp.float32)


def teacher_attention(context, w_out, tok_rows):
    tensor_size = lax.axis_size("tensor")
    partial = jnp.dot(context, w_out, preferred_element_type=jnp.float32).astype(jnp.bfloat16)
    if tensor_size != 2:
        return lax.psum_scatter(
            partial, "tensor", scatter_dimension=0, tiled=True
        ).astype(jnp.float32)
    me = lax.axis_index("tensor")
    halves = partial.reshape(2, tok_rows, partial.shape[1])
    mine = jnp.where(me == 0, halves[0], halves[1])
    theirs = jnp.where(me == 0, halves[1], halves[0])
    got = lax.ppermute(theirs, "tensor", perm=[(0, 1), (1, 0)])
    return mine.astype(jnp.float32) + got.astype(jnp.float32)


def local(
    context,
    w_out,
    teacher_input,
    teacher_gain,
    layer_weights,
    teacher_head,
    student_hidden,
    student_input,
    down_weight,
    student_gain,
    student_head,
    labels,
    lengths,
):
    tok_rows = teacher_input.shape[0]
    attention = teacher_attention(context, w_out, tok_rows)
    residual = teacher_input.astype(jnp.float32)
    layer_out = norm_rows(residual + attention, teacher_gain.astype(jnp.float32), teacher_eps)[0]
    blended = (layer_weights[0] * residual + layer_weights[1] * layer_out).astype(jnp.bfloat16)
    teacher_logits = jnp.dot(blended, teacher_head, preferred_element_type=jnp.float32)
    teacher_logp = jax.nn.log_softmax(teacher_logits, axis=-1)
    teacher_prob = jnp.exp(teacher_logp)
    ffn_out = folder(student_hidden, lax.all_gather(down_weight, TOKS, axis=0, tiled=True))
    student_scale = student_gain.astype(jnp.float32)
    normed, scaled, inverse = norm_rows(
        student_input.astype(jnp.float32) + ffn_out, student_scale, student_eps
    )
    features = normed.astype(jnp.bfloat16)
    student_logits = jnp.dot(features, student_head, preferred_element_type=jnp.float32)
    student_logp = jax.nn.log_softmax(student_logits, axis=-1)
    student_prob = jnp.exp(student_logp)
    first_token = lax.axis_index(TOKS) * tok_rows
    positions = first_token + jnp.arange(tok_rows, dtype=jnp.int32)
    sentence = positions // SEQ
    matches = sentence[:, None] == jnp.arange(lengths.shape[0], dtype=jnp.int32)[None, :]
    lengths_tok = jnp.sum(jnp.where(matches, lengths[None, :], 0), axis=1)
    validity = (positions % SEQ < lengths_tok).astype(jnp.float32)
    onehot = (
        labels[:, None] == jnp.arange(teacher_logits.shape[1], dtype=jnp.int32)[None, :]
    ).astype(jnp.float32)
    token_loss = jnp.sum(
        teacher_prob * (teacher_logp - student_logp), axis=1
    ) - label_weight * jnp.sum(onehot * student_logp, axis=1)
    loss_part = jnp.sum(validity * token_loss)
    logit_grad = (
        validity[:, None]
        * ((1.0 + label_weight) * student_prob - teacher_prob - label_weight * onehot)
    ).astype(jnp.bfloat16)
    head_term = lax.dot_general(
        features, logit_grad, (((0,), (0,)), ((), ())), preferred_element_type=jnp.float32
    )
    norm_grad = (
        jnp.dot(logit_grad, student_head.T, preferred_element_type=jnp.float32) * student_scale
    )
    grad_out = (
        (
            norm_grad
            - jnp.mean(norm_grad, axis=-1, keepdims=True)
            - scaled * jnp.mean(norm_grad * scaled, axis=-1, keepdims=True)
        )
        * inverse
    ).astype(jnp.bfloat16)
    group = lax.axis_size("g")
    hidden_cols = student_hidden.shape[1]
    hidden_split = student_hidden.reshape(tok_rows, group, hidden_cols // group)
    hidden_split = jnp.transpose(hidden_split, (1, 0, 2))
    hidden_mine = lax.all_to_all(hidden_split, "g", 0, 0, tiled=True)
    hidden_mine = hidden_mine.reshape(group * tok_rows, hidden_cols // group)
    grad_out_group = lax.all_gather(grad_out, "g", axis=0, tiled=True)
    grad_block = lax.dot_general(
        hidden_mine, grad_out_group, (((0,), (0,)), ((), ())), preferred_element_type=jnp.float32
    )
    grad_down = lax.psum_scatter(
        grad_block, ("c", "tensor"), scatter_dimension=0, tiled=True
    )
    classes = head_term.shape[1]
    packed = jnp.concatenate(
        [head_term.reshape(-1), jnp.stack([loss_part, jnp.sum(validity)])]
    )
    packed = lax.psum(packed, TOKS)
    head_total = packed[: head_term.size].reshape(-1, classes)
    return (grad_down, head_total, packed[head_term.size] / packed[head_term.size + 1])


def solution(mesh):
    dp = mesh.shape["dp"]
    tensor = mesh.shape["tensor"]
    devices = np.asarray(mesh.devices).reshape(dp // 2, 2, tensor)
    fine = Mesh(devices, TOKS)
    rows = P(TOKS, None)
    return jax.shard_map(
        local,
        mesh=fine,
        in_specs=(
            P(("g", "c"), "tensor"),
            P("tensor", None),
            rows,
            P(),
            P(),
            P(),
            rows,
            rows,
            rows,
            P(),
            P(),
            P(TOKS),
            P(),
        ),
        out_specs=(rows, P(), P()),
        check_vma=False,
    )
```

```python
import jax
import jax.numpy as jnp
import numpy as np
from jax import lax
from jax.sharding import Mesh
from jax.sharding import PartitionSpec as P

SEQ = 512


label_weight = 0.5
teacher_eps = 1e-05
student_eps = 1e-07

TOKS = ("g", "c", "tensor")


def norm_rows(values, gain_vec, epsilon):
    center = values - jnp.mean(values, axis=-1, keepdims=True)
    spread = jnp.mean(center * center, axis=-1, keepdims=True)
    inverse = lax.rsqrt(spread + epsilon)
    scaled = center * inverse
    return (scaled * gain_vec, scaled, inverse)


def folder(ordered, row_piece):
    return jnp.dot(ordered, row_piece, preferred_element_type=jnp.float32)


def teacher_attention(context, w_out, tok_rows):
    tensor_size = lax.axis_size("tensor")
    partial = jnp.dot(context, w_out, preferred_element_type=jnp.float32).astype(jnp.bfloat16)
    if tensor_size != 2:
        return lax.psum_scatter(
            partial, "tensor", scatter_dimension=0, tiled=True
        ).astype(jnp.float32)
    me = lax.axis_index("tensor")
    halves = partial.reshape(2, tok_rows, partial.shape[1])
    mine = jnp.where(me == 0, halves[0], halves[1])
    theirs = jnp.where(me == 0, halves[1], halves[0])
    got = lax.ppermute(theirs, "tensor", perm=[(0, 1), (1, 0)])
    return mine.astype(jnp.float32) + got.astype(jnp.float32)


def local(
    context,
    w_out,
    teacher_input,
    teacher_gain,
    layer_weights,
    teacher_head,
    student_hidden,
    student_input,
    down_weight,
    student_gain,
    student_head,
    labels,
    lengths,
):
    tok_rows = teacher_input.shape[0]
    attention = teacher_attention(context, w_out, tok_rows)
    residual = teacher_input.astype(jnp.float32)
    layer_out = norm_rows(residual + attention, teacher_gain.astype(jnp.float32), teacher_eps)[0]
    blended = (layer_weights[0] * residual + layer_weights[1] * layer_out).astype(jnp.bfloat16)
    teacher_logits = jnp.dot(blended, teacher_head, preferred_element_type=jnp.float32)
    teacher_logp = jax.nn.log_softmax(teacher_logits, axis=-1)
    teacher_prob = jnp.exp(teacher_logp)
    ffn_out = folder(student_hidden, lax.all_gather(down_weight, TOKS, axis=0, tiled=True))
    student_scale = student_gain.astype(jnp.float32)
    normed, scaled, inverse = norm_rows(
        student_input.astype(jnp.float32) + ffn_out, student_scale, student_eps
    )
    features = normed.astype(jnp.bfloat16)
    student_logits = jnp.dot(features, student_head, preferred_element_type=jnp.float32)
    student_logp = jax.nn.log_softmax(student_logits, axis=-1)
    student_prob = jnp.exp(student_logp)
    first_token = lax.axis_index(TOKS) * tok_rows
    positions = first_token + jnp.arange(tok_rows, dtype=jnp.int32)
    sentence = positions // SEQ
    matches = sentence[:, None] == jnp.arange(lengths.shape[0], dtype=jnp.int32)[None, :]
    lengths_tok = jnp.sum(jnp.where(matches, lengths[None, :], 0), axis=1)
    validity = (positions % SEQ < lengths_tok).astype(jnp.float32)
    onehot = (
        labels[:, None] == jnp.arange(teacher_logits.shape[1], dtype=jnp.int32)[None, :]
    ).astype(jnp.float32)
    token_loss = jnp.sum(
        teacher_prob * (teacher_logp - student_logp), axis=1
    ) - label_weight * jnp.sum(onehot * student_logp, axis=1)
    loss_part = jnp.sum(validity * token_loss)
    logit_grad = (
        validity[:, None]
        * ((1.0 + label_weight) * student_prob - teacher_prob - label_weight * onehot)
    ).astype(jnp.bfloat16)
    head_term = lax.dot_general(
        features, logit_grad, (((0,), (0,)), ((), ())), preferred_element_type=jnp.float32
    )
    norm_grad = (
        jnp.dot(logit_grad, student_head.T, preferred_element_type=jnp.float32) * student_scale
    )
    grad_out = (
        (
            norm_grad
            - jnp.mean(norm_grad, axis=-1, keepdims=True)
            - scaled * jnp.mean(norm_grad * scaled, axis=-1, keepdims=True)
        )
        * inverse
    ).astype(jnp.bfloat16)
    group = lax.axis_size("g")
    hidden_cols = student_hidden.shape[1]
    hidden_split = student_hidden.reshape(tok_rows, group, hidden_cols // group)
    hidden_split = jnp.transpose(hidden_split, (1, 0, 2))
    me = lax.axis_index("g")
    pieces = [hidden_split[me]]
    for k in range(1, group):
        send = lax.dynamic_index_in_dim(hidden_split, (me - k) % group, 0, keepdims=False)
        pieces.append(
            lax.ppermute(send, "g", perm=[(i, (i - k) % group) for i in range(group)])
        )
    hidden_mine = jnp.concatenate(pieces, axis=0)
    grad_out_group = lax.all_gather(grad_out, "g", axis=0, tiled=False)
    grad_out_group = jnp.roll(grad_out_group, -me, axis=0).reshape(group * tok_rows, -1)
    grad_block = lax.dot_general(
        hidden_mine, grad_out_group, (((0,), (0,)), ((), ())), preferred_element_type=jnp.float32
    )
    grad_down = lax.psum_scatter(
        grad_block, ("c", "tensor"), scatter_dimension=0, tiled=True
    )
    classes = head_term.shape[1]
    packed = jnp.concatenate(
        [head_term.reshape(-1), jnp.stack([loss_part, jnp.sum(validity)])]
    )
    packed = lax.psum(lax.psum(packed, "g"), ("c", "tensor"))
    head_total = packed[: head_term.size].reshape(-1, classes)
    return (grad_down, head_total, packed[head_term.size] / packed[head_term.size + 1])


def solution(mesh):
    dp = mesh.shape["dp"]
    tensor = mesh.shape["tensor"]
    devices = np.asarray(mesh.devices).reshape(dp // 2, 2, tensor)
    fine = Mesh(devices, TOKS)
    rows = P(TOKS, None)
    return jax.shard_map(
        local,
        mesh=fine,
        in_specs=(
            P(("g", "c"), "tensor"),
            P("tensor", None),
            rows,
            P(),
            P(),
            P(),
            rows,
            rows,
            rows,
            P(),
            P(),
            P(TOKS),
            P(),
        ),
        out_specs=(rows, P(), P()),
        check_vma=False,
    )
```

```python
import jax
import jax.numpy as jnp
import numpy as np
from jax import lax
from jax.sharding import Mesh
from jax.sharding import PartitionSpec as P

SEQ = 512


label_weight = 0.5
teacher_eps = 1e-05
student_eps = 1e-07

TOKS = ("g", "c", "tensor")


def norm_rows(values, gain_vec, epsilon):
    center = values - jnp.mean(values, axis=-1, keepdims=True)
    spread = jnp.mean(center * center, axis=-1, keepdims=True)
    inverse = lax.rsqrt(spread + epsilon)
    scaled = center * inverse
    return (scaled * gain_vec, scaled, inverse)


def folder(ordered, row_piece):
    return jnp.dot(ordered, row_piece, preferred_element_type=jnp.float32)


def teacher_attention(context, w_out, tok_rows):
    tensor_size = lax.axis_size("tensor")
    partial = jnp.dot(context, w_out, preferred_element_type=jnp.float32).astype(jnp.bfloat16)
    if tensor_size != 2:
        return lax.psum_scatter(
            partial, "tensor", scatter_dimension=0, tiled=True
        ).astype(jnp.float32)
    me = lax.axis_index("tensor")
    halves = partial.reshape(2, tok_rows, partial.shape[1])
    mine = jnp.where(me == 0, halves[0], halves[1])
    theirs = jnp.where(me == 0, halves[1], halves[0])
    got = lax.ppermute(theirs, "tensor", perm=[(0, 1), (1, 0)])
    return mine.astype(jnp.float32) + got.astype(jnp.float32)


def butterfly_sum(value, axes):
    for axis in axes:
        size = lax.axis_size(axis)
        if size & (size - 1):
            value = lax.psum(value, axis)
            continue
        step = 1
        while step < size:
            value = value + lax.ppermute(
                value, axis, perm=[(i, i ^ step) for i in range(size)]
            )
            step *= 2
    return value


def local(
    context,
    w_out,
    teacher_input,
    teacher_gain,
    layer_weights,
    teacher_head,
    student_hidden,
    student_input,
    down_weight,
    student_gain,
    student_head,
    labels,
    lengths,
):
    tok_rows = teacher_input.shape[0]
    attention = teacher_attention(context, w_out, tok_rows)
    residual = teacher_input.astype(jnp.float32)
    layer_out = norm_rows(residual + attention, teacher_gain.astype(jnp.float32), teacher_eps)[0]
    blended = (layer_weights[0] * residual + layer_weights[1] * layer_out).astype(jnp.bfloat16)
    teacher_logits = jnp.dot(blended, teacher_head, preferred_element_type=jnp.float32)
    teacher_logp = jax.nn.log_softmax(teacher_logits, axis=-1)
    teacher_prob = jnp.exp(teacher_logp)
    ffn_out = folder(student_hidden, lax.all_gather(down_weight, TOKS, axis=0, tiled=True))
    student_scale = student_gain.astype(jnp.float32)
    normed, scaled, inverse = norm_rows(
        student_input.astype(jnp.float32) + ffn_out, student_scale, student_eps
    )
    features = normed.astype(jnp.bfloat16)
    student_logits = jnp.dot(features, student_head, preferred_element_type=jnp.float32)
    student_logp = jax.nn.log_softmax(student_logits, axis=-1)
    student_prob = jnp.exp(student_logp)
    first_token = lax.axis_index(TOKS) * tok_rows
    positions = first_token + jnp.arange(tok_rows, dtype=jnp.int32)
    sentence = positions // SEQ
    matches = sentence[:, None] == jnp.arange(lengths.shape[0], dtype=jnp.int32)[None, :]
    lengths_tok = jnp.sum(jnp.where(matches, lengths[None, :], 0), axis=1)
    validity = (positions % SEQ < lengths_tok).astype(jnp.float32)
    onehot = (
        labels[:, None] == jnp.arange(teacher_logits.shape[1], dtype=jnp.int32)[None, :]
    ).astype(jnp.float32)
    token_loss = jnp.sum(
        teacher_prob * (teacher_logp - student_logp), axis=1
    ) - label_weight * jnp.sum(onehot * student_logp, axis=1)
    loss_part = jnp.sum(validity * token_loss)
    logit_grad = (
        validity[:, None]
        * ((1.0 + label_weight) * student_prob - teacher_prob - label_weight * onehot)
    ).astype(jnp.bfloat16)
    head_term = lax.dot_general(
        features, logit_grad, (((0,), (0,)), ((), ())), preferred_element_type=jnp.float32
    )
    norm_grad = (
        jnp.dot(logit_grad, student_head.T, preferred_element_type=jnp.float32) * student_scale
    )
    grad_out = (
        (
            norm_grad
            - jnp.mean(norm_grad, axis=-1, keepdims=True)
            - scaled * jnp.mean(norm_grad * scaled, axis=-1, keepdims=True)
        )
        * inverse
    ).astype(jnp.bfloat16)
    group = lax.axis_size("g")
    hidden_cols = student_hidden.shape[1]
    hidden_split = student_hidden.reshape(tok_rows, group, hidden_cols // group)
    hidden_split = jnp.transpose(hidden_split, (1, 0, 2))
    me = lax.axis_index("g")
    pieces = [hidden_split[me]]
    for k in range(1, group):
        send = lax.dynamic_index_in_dim(hidden_split, (me - k) % group, 0, keepdims=False)
        pieces.append(
            lax.ppermute(send, "g", perm=[(i, (i - k) % group) for i in range(group)])
        )
    hidden_mine = jnp.concatenate(pieces, axis=0)
    grad_out_group = lax.all_gather(grad_out, "g", axis=0, tiled=False)
    grad_out_group = jnp.roll(grad_out_group, -me, axis=0).reshape(group * tok_rows, -1)
    grad_block = lax.dot_general(
        hidden_mine, grad_out_group, (((0,), (0,)), ((), ())), preferred_element_type=jnp.float32
    )
    grad_down = lax.psum_scatter(
        grad_block, ("c", "tensor"), scatter_dimension=0, tiled=True
    )
    classes = head_term.shape[1]
    packed = jnp.concatenate(
        [head_term.reshape(-1), jnp.stack([loss_part, jnp.sum(validity)])]
    )
    packed = butterfly_sum(packed, ("tensor", "c", "g"))
    head_total = packed[: head_term.size].reshape(-1, classes)
    return (grad_down, head_total, packed[head_term.size] / packed[head_term.size + 1])


def solution(mesh):
    dp = mesh.shape["dp"]
    tensor = mesh.shape["tensor"]
    devices = np.asarray(mesh.devices).reshape(dp // 2, 2, tensor)
    fine = Mesh(devices, TOKS)
    rows = P(TOKS, None)
    return jax.shard_map(
        local,
        mesh=fine,
        in_specs=(
            P(("g", "c"), "tensor"),
            P("tensor", None),
            rows,
            P(),
            P(),
            P(),
            rows,
            rows,
            rows,
            P(),
            P(),
            P(TOKS),
            P(),
        ),
        out_specs=(rows, P(), P()),
        check_vma=False,
    )
```

```python
import jax
import jax.numpy as jnp
import numpy as np
from jax import lax
from jax.sharding import Mesh
from jax.sharding import PartitionSpec as P

SEQ = 512


label_weight = 0.5
teacher_eps = 1e-05
student_eps = 1e-07

TOKS = ("g", "c", "tensor")


def norm_rows(values, gain_vec, epsilon):
    center = values - jnp.mean(values, axis=-1, keepdims=True)
    spread = jnp.mean(center * center, axis=-1, keepdims=True)
    inverse = lax.rsqrt(spread + epsilon)
    scaled = center * inverse
    return (scaled * gain_vec, scaled, inverse)


def folder(ordered, row_piece):
    return jnp.dot(ordered, row_piece, preferred_element_type=jnp.float32)


def teacher_attention(context, w_out, tok_rows):
    tensor_size = lax.axis_size("tensor")
    partial = jnp.dot(context, w_out, preferred_element_type=jnp.float32).astype(jnp.bfloat16)
    if tensor_size != 2:
        return lax.psum_scatter(
            partial, "tensor", scatter_dimension=0, tiled=True
        ).astype(jnp.float32)
    me = lax.axis_index("tensor")
    halves = partial.reshape(2, tok_rows, partial.shape[1])
    mine = jnp.where(me == 0, halves[0], halves[1])
    theirs = jnp.where(me == 0, halves[1], halves[0])
    got = lax.ppermute(theirs, "tensor", perm=[(0, 1), (1, 0)])
    return mine.astype(jnp.float32) + got.astype(jnp.float32)


def butterfly_sum(value, axes):
    for axis in axes:
        size = lax.axis_size(axis)
        if size & (size - 1):
            value = lax.psum(value, axis)
            continue
        step = 1
        while step < size:
            value = value + lax.ppermute(
                value, axis, perm=[(i, i ^ step) for i in range(size)]
            )
            step *= 2
    return value


def butterfly_gather(value, axes):
    for axis in reversed(axes):
        size = lax.axis_size(axis)
        me = lax.axis_index(axis)
        step = 1
        while step < size:
            got = lax.ppermute(value, axis, perm=[(i, i ^ step) for i in range(size)])
            low = (me & step) == 0
            value = jnp.where(
                low, jnp.concatenate([value, got], 0), jnp.concatenate([got, value], 0)
            )
            step *= 2
    return value


def split_gather(value, axes):
    half = value.shape[1] // 2
    pow2 = all((lax.axis_size(a) & (lax.axis_size(a) - 1)) == 0 for a in axes)
    if not pow2 or half % 128:
        return (lax.all_gather(value, axes, axis=0, tiled=True),)
    return (
        lax.all_gather(value[:, :half], axes, axis=0, tiled=True),
        butterfly_gather(value[:, half:], axes),
    )


def local(
    context,
    w_out,
    teacher_input,
    teacher_gain,
    layer_weights,
    teacher_head,
    student_hidden,
    student_input,
    down_weight,
    student_gain,
    student_head,
    labels,
    lengths,
):
    tok_rows = teacher_input.shape[0]
    attention = teacher_attention(context, w_out, tok_rows)
    residual = teacher_input.astype(jnp.float32)
    layer_out = norm_rows(residual + attention, teacher_gain.astype(jnp.float32), teacher_eps)[0]
    blended = (layer_weights[0] * residual + layer_weights[1] * layer_out).astype(jnp.bfloat16)
    teacher_logits = jnp.dot(blended, teacher_head, preferred_element_type=jnp.float32)
    teacher_logp = jax.nn.log_softmax(teacher_logits, axis=-1)
    teacher_prob = jnp.exp(teacher_logp)
    ffn_out = jnp.concatenate(
        [folder(student_hidden, part) for part in split_gather(down_weight, TOKS)], axis=1
    )
    student_scale = student_gain.astype(jnp.float32)
    normed, scaled, inverse = norm_rows(
        student_input.astype(jnp.float32) + ffn_out, student_scale, student_eps
    )
    features = normed.astype(jnp.bfloat16)
    student_logits = jnp.dot(features, student_head, preferred_element_type=jnp.float32)
    student_logp = jax.nn.log_softmax(student_logits, axis=-1)
    student_prob = jnp.exp(student_logp)
    first_token = lax.axis_index(TOKS) * tok_rows
    positions = first_token + jnp.arange(tok_rows, dtype=jnp.int32)
    sentence = positions // SEQ
    matches = sentence[:, None] == jnp.arange(lengths.shape[0], dtype=jnp.int32)[None, :]
    lengths_tok = jnp.sum(jnp.where(matches, lengths[None, :], 0), axis=1)
    validity = (positions % SEQ < lengths_tok).astype(jnp.float32)
    onehot = (
        labels[:, None] == jnp.arange(teacher_logits.shape[1], dtype=jnp.int32)[None, :]
    ).astype(jnp.float32)
    token_loss = jnp.sum(
        teacher_prob * (teacher_logp - student_logp), axis=1
    ) - label_weight * jnp.sum(onehot * student_logp, axis=1)
    loss_part = jnp.sum(validity * token_loss)
    logit_grad = (
        validity[:, None]
        * ((1.0 + label_weight) * student_prob - teacher_prob - label_weight * onehot)
    ).astype(jnp.bfloat16)
    head_term = lax.dot_general(
        features, logit_grad, (((0,), (0,)), ((), ())), preferred_element_type=jnp.float32
    )
    norm_grad = (
        jnp.dot(logit_grad, student_head.T, preferred_element_type=jnp.float32) * student_scale
    )
    grad_out = (
        (
            norm_grad
            - jnp.mean(norm_grad, axis=-1, keepdims=True)
            - scaled * jnp.mean(norm_grad * scaled, axis=-1, keepdims=True)
        )
        * inverse
    ).astype(jnp.bfloat16)
    group = lax.axis_size("g")
    hidden_cols = student_hidden.shape[1]
    hidden_split = student_hidden.reshape(tok_rows, group, hidden_cols // group)
    hidden_split = jnp.transpose(hidden_split, (1, 0, 2))
    me = lax.axis_index("g")
    pieces = [hidden_split[me]]
    for k in range(1, group):
        send = lax.dynamic_index_in_dim(hidden_split, (me - k) % group, 0, keepdims=False)
        pieces.append(
            lax.ppermute(send, "g", perm=[(i, (i - k) % group) for i in range(group)])
        )
    hidden_mine = jnp.concatenate(pieces, axis=0)
    grad_out_parts = split_gather(grad_out, ("g",))
    grad_block = jnp.concatenate(
        [
            lax.dot_general(
                hidden_mine,
                jnp.roll(part, -me * tok_rows, axis=0),
                (((0,), (0,)), ((), ())),
                preferred_element_type=jnp.float32,
            )
            for part in grad_out_parts
        ],
        axis=1,
    )
    grad_down = lax.psum_scatter(
        grad_block, ("c", "tensor"), scatter_dimension=0, tiled=True
    )
    classes = head_term.shape[1]
    packed = jnp.concatenate(
        [head_term.reshape(-1), jnp.stack([loss_part, jnp.sum(validity)])]
    )
    packed = butterfly_sum(packed, ("tensor", "c", "g"))
    head_total = packed[: head_term.size].reshape(-1, classes)
    return (grad_down, head_total, packed[head_term.size] / packed[head_term.size + 1])


def solution(mesh):
    dp = mesh.shape["dp"]
    tensor = mesh.shape["tensor"]
    devices = np.asarray(mesh.devices).reshape(dp // 2, 2, tensor)
    fine = Mesh(devices, TOKS)
    rows = P(TOKS, None)
    return jax.shard_map(
        local,
        mesh=fine,
        in_specs=(
            P(("g", "c"), "tensor"),
            P("tensor", None),
            rows,
            P(),
            P(),
            P(),
            rows,
            rows,
            rows,
            P(),
            P(),
            P(TOKS),
            P(),
        ),
        out_specs=(rows, P(), P()),
        check_vma=False,
    )
```

```python
import jax
import jax.numpy as jnp
import numpy as np
from jax import lax
from jax.sharding import Mesh
from jax.sharding import PartitionSpec as P

SEQ = 512


label_weight = 0.5
teacher_eps = 1e-05
student_eps = 1e-07

TOKS = ("g", "c", "tensor")


def norm_rows(values, gain_vec, epsilon):
    center = values - jnp.mean(values, axis=-1, keepdims=True)
    spread = jnp.mean(center * center, axis=-1, keepdims=True)
    inverse = lax.rsqrt(spread + epsilon)
    scaled = center * inverse
    return (scaled * gain_vec, scaled, inverse)


def folder(ordered, row_piece):
    return jnp.dot(ordered, row_piece, preferred_element_type=jnp.float32)


def teacher_attention(context, w_out, tok_rows):
    tensor_size = lax.axis_size("tensor")
    partial = jnp.dot(context, w_out, preferred_element_type=jnp.float32).astype(jnp.bfloat16)
    if tensor_size != 2:
        return lax.psum_scatter(
            partial, "tensor", scatter_dimension=0, tiled=True
        ).astype(jnp.float32)
    me = lax.axis_index("tensor")
    halves = partial.reshape(2, tok_rows, partial.shape[1])
    mine = jnp.where(me == 0, halves[0], halves[1])
    theirs = jnp.where(me == 0, halves[1], halves[0])
    got = lax.ppermute(theirs, "tensor", perm=[(0, 1), (1, 0)])
    return mine.astype(jnp.float32) + got.astype(jnp.float32)


def butterfly_sum(value, axes):
    for axis in axes:
        size = lax.axis_size(axis)
        if size & (size - 1):
            value = lax.psum(value, axis)
            continue
        step = 1
        while step < size:
            value = value + lax.ppermute(
                value, axis, perm=[(i, i ^ step) for i in range(size)]
            )
            step *= 2
    return value


def local(
    context,
    w_out,
    teacher_input,
    teacher_gain,
    layer_weights,
    teacher_head,
    student_hidden,
    student_input,
    down_weight,
    student_gain,
    student_head,
    labels,
    lengths,
):
    tok_rows = teacher_input.shape[0]
    attention = teacher_attention(context, w_out, tok_rows)
    group = lax.axis_size("g")
    hidden_cols = student_hidden.shape[1]
    hidden_split = student_hidden.reshape(tok_rows, group, hidden_cols // group)
    hidden_split = jnp.transpose(hidden_split, (1, 0, 2))
    me = lax.axis_index("g")
    pieces = [hidden_split[me]]
    for k in range(1, group):
        send = lax.dynamic_index_in_dim(hidden_split, (me - k) % group, 0, keepdims=False)
        pieces.append(
            lax.ppermute(send, "g", perm=[(i, (i - k) % group) for i in range(group)])
        )
    hidden_mine = jnp.concatenate(pieces, axis=0)
    hidden_mine, attention = lax.optimization_barrier((hidden_mine, attention))
    residual = teacher_input.astype(jnp.float32)
    layer_out = norm_rows(residual + attention, teacher_gain.astype(jnp.float32), teacher_eps)[0]
    blended = (layer_weights[0] * residual + layer_weights[1] * layer_out).astype(jnp.bfloat16)
    teacher_logits = jnp.dot(blended, teacher_head, preferred_element_type=jnp.float32)
    teacher_logp = jax.nn.log_softmax(teacher_logits, axis=-1)
    teacher_prob = jnp.exp(teacher_logp)
    ffn_out = folder(student_hidden, lax.all_gather(down_weight, TOKS, axis=0, tiled=True))
    student_scale = student_gain.astype(jnp.float32)
    normed, scaled, inverse = norm_rows(
        student_input.astype(jnp.float32) + ffn_out, student_scale, student_eps
    )
    features = normed.astype(jnp.bfloat16)
    student_logits = jnp.dot(features, student_head, preferred_element_type=jnp.float32)
    student_logp = jax.nn.log_softmax(student_logits, axis=-1)
    student_prob = jnp.exp(student_logp)
    first_token = lax.axis_index(TOKS) * tok_rows
    positions = first_token + jnp.arange(tok_rows, dtype=jnp.int32)
    sentence = positions // SEQ
    matches = sentence[:, None] == jnp.arange(lengths.shape[0], dtype=jnp.int32)[None, :]
    lengths_tok = jnp.sum(jnp.where(matches, lengths[None, :], 0), axis=1)
    validity = (positions % SEQ < lengths_tok).astype(jnp.float32)
    onehot = (
        labels[:, None] == jnp.arange(teacher_logits.shape[1], dtype=jnp.int32)[None, :]
    ).astype(jnp.float32)
    token_loss = jnp.sum(
        teacher_prob * (teacher_logp - student_logp), axis=1
    ) - label_weight * jnp.sum(onehot * student_logp, axis=1)
    loss_part = jnp.sum(validity * token_loss)
    logit_grad = (
        validity[:, None]
        * ((1.0 + label_weight) * student_prob - teacher_prob - label_weight * onehot)
    ).astype(jnp.bfloat16)
    head_term = lax.dot_general(
        features, logit_grad, (((0,), (0,)), ((), ())), preferred_element_type=jnp.float32
    )
    norm_grad = (
        jnp.dot(logit_grad, student_head.T, preferred_element_type=jnp.float32) * student_scale
    )
    grad_out = (
        (
            norm_grad
            - jnp.mean(norm_grad, axis=-1, keepdims=True)
            - scaled * jnp.mean(norm_grad * scaled, axis=-1, keepdims=True)
        )
        * inverse
    ).astype(jnp.bfloat16)
    grad_out_group = jnp.concatenate(
        [grad_out]
        + [
            lax.ppermute(grad_out, "g", perm=[(i, (i - k) % group) for i in range(group)])
            for k in range(1, group)
        ],
        axis=0,
    )
    grad_block = lax.dot_general(
        hidden_mine, grad_out_group, (((0,), (0,)), ((), ())), preferred_element_type=jnp.float32
    )
    grad_down = lax.psum_scatter(
        grad_block, ("c", "tensor"), scatter_dimension=0, tiled=True
    )
    classes = head_term.shape[1]
    packed = jnp.concatenate(
        [head_term.reshape(-1), jnp.stack([loss_part, jnp.sum(validity)])]
    )
    packed = butterfly_sum(packed, ("tensor", "c", "g"))
    head_total = packed[: head_term.size].reshape(-1, classes)
    return (grad_down, head_total, packed[head_term.size] / packed[head_term.size + 1])


def solution(mesh):
    dp = mesh.shape["dp"]
    tensor = mesh.shape["tensor"]
    devices = np.asarray(mesh.devices).reshape(dp // 2, 2, tensor)
    fine = Mesh(devices, TOKS)
    rows = P(TOKS, None)
    return jax.shard_map(
        local,
        mesh=fine,
        in_specs=(
            P(("g", "c"), "tensor"),
            P("tensor", None),
            rows,
            P(),
            P(),
            P(),
            rows,
            rows,
            rows,
            P(),
            P(),
            P(TOKS),
            P(),
        ),
        out_specs=(rows, P(), P()),
        check_vma=False,
    )
```

```python
import jax
import jax.numpy as jnp
import numpy as np
from jax import lax
from jax.sharding import Mesh
from jax.sharding import PartitionSpec as P

SEQ = 512


label_weight = 0.5
teacher_eps = 1e-05
student_eps = 1e-07

TOKS = ("q", "x", "c", "tensor")
GROUP = ("x", "c", "tensor")


def norm_rows(values, gain_vec, epsilon):
    center = values - jnp.mean(values, axis=-1, keepdims=True)
    spread = jnp.mean(center * center, axis=-1, keepdims=True)
    inverse = lax.rsqrt(spread + epsilon)
    scaled = center * inverse
    return (scaled * gain_vec, scaled, inverse)


def folder(ordered, row_piece):
    return jnp.dot(ordered, row_piece, preferred_element_type=jnp.float32)


def teacher_attention(context, w_out, tok_rows):
    tensor_size = lax.axis_size("tensor")
    partial = jnp.dot(context, w_out, preferred_element_type=jnp.float32).astype(jnp.bfloat16)
    if tensor_size != 2:
        return lax.psum_scatter(
            partial, "tensor", scatter_dimension=0, tiled=True
        ).astype(jnp.float32)
    me = lax.axis_index("tensor")
    halves = partial.reshape(2, tok_rows, partial.shape[1])
    mine = jnp.where(me == 0, halves[0], halves[1])
    theirs = jnp.where(me == 0, halves[1], halves[0])
    got = lax.ppermute(theirs, "tensor", perm=[(0, 1), (1, 0)])
    return mine.astype(jnp.float32) + got.astype(jnp.float32)


def butterfly_sum(value, axes):
    for axis in axes:
        size = lax.axis_size(axis)
        if size & (size - 1):
            value = lax.psum(value, axis)
            continue
        step = 1
        while step < size:
            value = value + lax.ppermute(
                value, axis, perm=[(i, i ^ step) for i in range(size)]
            )
            step *= 2
    return value


def local(
    context,
    w_out,
    teacher_input,
    teacher_gain,
    layer_weights,
    teacher_head,
    student_hidden,
    student_input,
    down_weight,
    student_gain,
    student_head,
    labels,
    lengths,
):
    tok_rows = teacher_input.shape[0]
    attention = teacher_attention(context, w_out, tok_rows)
    group = lax.axis_size(GROUP)
    outer = lax.axis_size("q")
    hidden_cols = student_hidden.shape[1]
    block = hidden_cols // (group * outer)
    hidden_split = student_hidden.reshape(tok_rows, outer, group, block)
    hidden_split = jnp.transpose(hidden_split, (2, 0, 1, 3)).reshape(group, tok_rows, outer * block)
    me = lax.axis_index(GROUP)
    pieces = [hidden_split[me]]
    for k in range(1, group):
        send = lax.dynamic_index_in_dim(hidden_split, (me - k) % group, 0, keepdims=False)
        pieces.append(
            lax.ppermute(send, GROUP, perm=[(i, (i - k) % group) for i in range(group)])
        )
    hidden_mine = jnp.concatenate(pieces, axis=0)
    hidden_mine, attention = lax.optimization_barrier((hidden_mine, attention))
    residual = teacher_input.astype(jnp.float32)
    layer_out = norm_rows(residual + attention, teacher_gain.astype(jnp.float32), teacher_eps)[0]
    blended = (layer_weights[0] * residual + layer_weights[1] * layer_out).astype(jnp.bfloat16)
    teacher_logits = jnp.dot(blended, teacher_head, preferred_element_type=jnp.float32)
    teacher_logp = jax.nn.log_softmax(teacher_logits, axis=-1)
    teacher_prob = jnp.exp(teacher_logp)
    ffn_out = folder(student_hidden, lax.all_gather(down_weight, TOKS, axis=0, tiled=True))
    student_scale = student_gain.astype(jnp.float32)
    normed, scaled, inverse = norm_rows(
        student_input.astype(jnp.float32) + ffn_out, student_scale, student_eps
    )
    features = normed.astype(jnp.bfloat16)
    student_logits = jnp.dot(features, student_head, preferred_element_type=jnp.float32)
    student_logp = jax.nn.log_softmax(student_logits, axis=-1)
    student_prob = jnp.exp(student_logp)
    first_token = lax.axis_index(TOKS) * tok_rows
    positions = first_token + jnp.arange(tok_rows, dtype=jnp.int32)
    sentence = positions // SEQ
    matches = sentence[:, None] == jnp.arange(lengths.shape[0], dtype=jnp.int32)[None, :]
    lengths_tok = jnp.sum(jnp.where(matches, lengths[None, :], 0), axis=1)
    validity = (positions % SEQ < lengths_tok).astype(jnp.float32)
    onehot = (
        labels[:, None] == jnp.arange(teacher_logits.shape[1], dtype=jnp.int32)[None, :]
    ).astype(jnp.float32)
    token_loss = jnp.sum(
        teacher_prob * (teacher_logp - student_logp), axis=1
    ) - label_weight * jnp.sum(onehot * student_logp, axis=1)
    loss_part = jnp.sum(validity * token_loss)
    logit_grad = (
        validity[:, None]
        * ((1.0 + label_weight) * student_prob - teacher_prob - label_weight * onehot)
    ).astype(jnp.bfloat16)
    head_term = lax.dot_general(
        features, logit_grad, (((0,), (0,)), ((), ())), preferred_element_type=jnp.float32
    )
    norm_grad = (
        jnp.dot(logit_grad, student_head.T, preferred_element_type=jnp.float32) * student_scale
    )
    grad_out = (
        (
            norm_grad
            - jnp.mean(norm_grad, axis=-1, keepdims=True)
            - scaled * jnp.mean(norm_grad * scaled, axis=-1, keepdims=True)
        )
        * inverse
    ).astype(jnp.bfloat16)
    grad_out_group = jnp.concatenate(
        [grad_out]
        + [
            lax.ppermute(grad_out, GROUP, perm=[(i, (i - k) % group) for i in range(group)])
            for k in range(1, group)
        ],
        axis=0,
    )
    grad_block = lax.dot_general(
        hidden_mine, grad_out_group, (((0,), (0,)), ((), ())), preferred_element_type=jnp.float32
    )
    grad_down = lax.psum_scatter(
        grad_block, "q", scatter_dimension=0, tiled=True
    )
    classes = head_term.shape[1]
    packed = jnp.concatenate(
        [head_term.reshape(-1), jnp.stack([loss_part, jnp.sum(validity)])]
    )
    packed = butterfly_sum(packed, ("tensor", "c", "x", "q"))
    head_total = packed[: head_term.size].reshape(-1, classes)
    return (grad_down, head_total, packed[head_term.size] / packed[head_term.size + 1])


def solution(mesh):
    dp = mesh.shape["dp"]
    tensor = mesh.shape["tensor"]
    devices = np.asarray(mesh.devices).reshape(dp // 4, 2, 2, tensor)
    fine = Mesh(devices, TOKS)
    rows = P(TOKS, None)
    return jax.shard_map(
        local,
        mesh=fine,
        in_specs=(
            P(("q", "x", "c"), "tensor"),
            P("tensor", None),
            rows,
            P(),
            P(),
            P(),
            rows,
            rows,
            rows,
            P(),
            P(),
            P(TOKS),
            P(),
        ),
        out_specs=(rows, P(), P()),
        check_vma=False,
    )
```

```python
import jax
import jax.numpy as jnp
import numpy as np
from jax import lax
from jax.sharding import Mesh
from jax.sharding import PartitionSpec as P

SEQ = 512


label_weight = 0.5
teacher_eps = 1e-05
student_eps = 1e-07

TOKS = ("q", "x", "c", "tensor")
GROUP = ("x", "c", "tensor")


def norm_rows(values, gain_vec, epsilon):
    center = values - jnp.mean(values, axis=-1, keepdims=True)
    spread = jnp.mean(center * center, axis=-1, keepdims=True)
    inverse = lax.rsqrt(spread + epsilon)
    scaled = center * inverse
    return (scaled * gain_vec, scaled, inverse)


def folder(ordered, row_piece):
    return jnp.dot(ordered, row_piece, preferred_element_type=jnp.float32)


def teacher_attention(context, w_out, tok_rows):
    tensor_size = lax.axis_size("tensor")
    partial = jnp.dot(context, w_out, preferred_element_type=jnp.float32).astype(jnp.bfloat16)
    if tensor_size != 2:
        return lax.psum_scatter(
            partial, "tensor", scatter_dimension=0, tiled=True
        ).astype(jnp.float32)
    me = lax.axis_index("tensor")
    halves = partial.reshape(2, tok_rows, partial.shape[1])
    mine = jnp.where(me == 0, halves[0], halves[1])
    theirs = jnp.where(me == 0, halves[1], halves[0])
    got = lax.ppermute(theirs, "tensor", perm=[(0, 1), (1, 0)])
    return mine.astype(jnp.float32) + got.astype(jnp.float32)


def butterfly_sum(value, axes):
    for axis in axes:
        size = lax.axis_size(axis)
        if size & (size - 1):
            value = lax.psum(value, axis)
            continue
        step = 1
        while step < size:
            value = value + lax.ppermute(
                value, axis, perm=[(i, i ^ step) for i in range(size)]
            )
            step *= 2
    return value


def local(
    context,
    w_out,
    teacher_input,
    teacher_gain,
    layer_weights,
    teacher_head,
    student_hidden,
    student_input,
    down_weight,
    student_gain,
    student_head,
    labels,
    lengths,
):
    tok_rows = teacher_input.shape[0]
    attention = teacher_attention(context, w_out, tok_rows)
    group = lax.axis_size(GROUP)
    outer = lax.axis_size("q")
    hidden_cols = student_hidden.shape[1]
    block = hidden_cols // (group * outer)
    hidden_split = student_hidden.reshape(tok_rows, outer, group, block)
    hidden_split = jnp.transpose(hidden_split, (2, 0, 1, 3)).reshape(group, tok_rows, outer * block)
    me = lax.axis_index(GROUP)
    pieces = [hidden_split[me]]
    for k in range(1, group):
        send = lax.dynamic_index_in_dim(hidden_split, (me - k) % group, 0, keepdims=False)
        pieces.append(
            lax.ppermute(send, GROUP, perm=[(i, (i - k) % group) for i in range(group)])
        )
    hidden_mine = jnp.concatenate(pieces, axis=0)
    hidden_mine, attention = lax.optimization_barrier((hidden_mine, attention))
    residual = teacher_input.astype(jnp.float32)
    layer_out = norm_rows(residual + attention, teacher_gain.astype(jnp.float32), teacher_eps)[0]
    blended = (layer_weights[0] * residual + layer_weights[1] * layer_out).astype(jnp.bfloat16)
    teacher_logits = jnp.dot(blended, teacher_head, preferred_element_type=jnp.float32)
    teacher_logp = jax.nn.log_softmax(teacher_logits, axis=-1)
    teacher_prob = jnp.exp(teacher_logp)
    per_core = lax.all_gather(down_weight, ("q", "x", "tensor"), axis=0, tiled=True)
    other_core = lax.ppermute(per_core, "c", perm=[(0, 1), (1, 0)])
    core = lax.axis_index("c")
    by_core = student_hidden.reshape(
        tok_rows, -1, 2, lax.axis_size("tensor") * down_weight.shape[0]
    )
    hidden_mine_core = lax.dynamic_index_in_dim(by_core, core, 2, keepdims=False)
    hidden_other_core = lax.dynamic_index_in_dim(by_core, 1 - core, 2, keepdims=False)
    ffn_out = folder(hidden_mine_core.reshape(tok_rows, -1), per_core) + folder(
        hidden_other_core.reshape(tok_rows, -1), other_core
    )
    student_scale = student_gain.astype(jnp.float32)
    normed, scaled, inverse = norm_rows(
        student_input.astype(jnp.float32) + ffn_out, student_scale, student_eps
    )
    features = normed.astype(jnp.bfloat16)
    student_logits = jnp.dot(features, student_head, preferred_element_type=jnp.float32)
    student_logp = jax.nn.log_softmax(student_logits, axis=-1)
    student_prob = jnp.exp(student_logp)
    first_token = lax.axis_index(TOKS) * tok_rows
    positions = first_token + jnp.arange(tok_rows, dtype=jnp.int32)
    sentence = positions // SEQ
    matches = sentence[:, None] == jnp.arange(lengths.shape[0], dtype=jnp.int32)[None, :]
    lengths_tok = jnp.sum(jnp.where(matches, lengths[None, :], 0), axis=1)
    validity = (positions % SEQ < lengths_tok).astype(jnp.float32)
    onehot = (
        labels[:, None] == jnp.arange(teacher_logits.shape[1], dtype=jnp.int32)[None, :]
    ).astype(jnp.float32)
    token_loss = jnp.sum(
        teacher_prob * (teacher_logp - student_logp), axis=1
    ) - label_weight * jnp.sum(onehot * student_logp, axis=1)
    loss_part = jnp.sum(validity * token_loss)
    logit_grad = (
        validity[:, None]
        * ((1.0 + label_weight) * student_prob - teacher_prob - label_weight * onehot)
    ).astype(jnp.bfloat16)
    head_term = lax.dot_general(
        features, logit_grad, (((0,), (0,)), ((), ())), preferred_element_type=jnp.float32
    )
    norm_grad = (
        jnp.dot(logit_grad, student_head.T, preferred_element_type=jnp.float32) * student_scale
    )
    grad_out = (
        (
            norm_grad
            - jnp.mean(norm_grad, axis=-1, keepdims=True)
            - scaled * jnp.mean(norm_grad * scaled, axis=-1, keepdims=True)
        )
        * inverse
    ).astype(jnp.bfloat16)
    grad_out_group = jnp.concatenate(
        [grad_out]
        + [
            lax.ppermute(grad_out, GROUP, perm=[(i, (i - k) % group) for i in range(group)])
            for k in range(1, group)
        ],
        axis=0,
    )
    grad_block = lax.dot_general(
        hidden_mine, grad_out_group, (((0,), (0,)), ((), ())), preferred_element_type=jnp.float32
    )
    grad_down = lax.psum_scatter(
        grad_block, "q", scatter_dimension=0, tiled=True
    )
    classes = head_term.shape[1]
    packed = jnp.concatenate(
        [head_term.reshape(-1), jnp.stack([loss_part, jnp.sum(validity)])]
    )
    packed = butterfly_sum(packed, ("tensor", "c", "x", "q"))
    head_total = packed[: head_term.size].reshape(-1, classes)
    return (grad_down, head_total, packed[head_term.size] / packed[head_term.size + 1])


def solution(mesh):
    dp = mesh.shape["dp"]
    tensor = mesh.shape["tensor"]
    devices = np.asarray(mesh.devices).reshape(dp // 4, 2, 2, tensor)
    fine = Mesh(devices, TOKS)
    rows = P(TOKS, None)
    return jax.shard_map(
        local,
        mesh=fine,
        in_specs=(
            P(("q", "x", "c"), "tensor"),
            P("tensor", None),
            rows,
            P(),
            P(),
            P(),
            rows,
            rows,
            rows,
            P(),
            P(),
            P(TOKS),
            P(),
        ),
        out_specs=(rows, P(), P()),
        check_vma=False,
    )
```

```python
import jax
import jax.numpy as jnp
import numpy as np
from jax import lax
from jax.sharding import Mesh
from jax.sharding import PartitionSpec as P

SEQ = 512


label_weight = 0.5
teacher_eps = 1e-05
student_eps = 1e-07

TOKS = ("q", "x", "c", "tensor")
GROUP = ("x", "c", "tensor")


def norm_rows(values, gain_vec, epsilon):
    center = values - jnp.mean(values, axis=-1, keepdims=True)
    spread = jnp.mean(center * center, axis=-1, keepdims=True)
    inverse = lax.rsqrt(spread + epsilon)
    scaled = center * inverse
    return (scaled * gain_vec, scaled, inverse)


def folder(ordered, row_piece):
    return jnp.dot(ordered, row_piece, preferred_element_type=jnp.float32)


def teacher_attention(context, w_out, tok_rows):
    tensor_size = lax.axis_size("tensor")
    partial = jnp.dot(context, w_out, preferred_element_type=jnp.float32).astype(jnp.bfloat16)
    if tensor_size != 2:
        return lax.psum_scatter(
            partial, "tensor", scatter_dimension=0, tiled=True
        ).astype(jnp.float32)
    me = lax.axis_index("tensor")
    halves = partial.reshape(2, tok_rows, partial.shape[1])
    mine = jnp.where(me == 0, halves[0], halves[1])
    theirs = jnp.where(me == 0, halves[1], halves[0])
    got = lax.ppermute(theirs, "tensor", perm=[(0, 1), (1, 0)])
    return mine.astype(jnp.float32) + got.astype(jnp.float32)


def butterfly_sum(value, axes):
    for axis in axes:
        size = lax.axis_size(axis)
        if size & (size - 1):
            value = lax.psum(value, axis)
            continue
        step = 1
        while step < size:
            value = value + lax.ppermute(
                value, axis, perm=[(i, i ^ step) for i in range(size)]
            )
            step *= 2
    return value


def group_gather(value):
    chips = ("x", "tensor")
    n = lax.axis_size(chips)
    j = lax.axis_index(chips)
    parts = [value] + [
        lax.ppermute(value, chips, perm=[(i, (i - k) % n) for i in range(n)])
        for k in range(1, n)
    ]
    plane = jnp.roll(jnp.stack(parts), j, axis=0)
    other = lax.ppermute(plane, "c", perm=[(0, 1), (1, 0)])
    low = lax.axis_index("c") == 0
    both = jnp.where(low, jnp.stack([plane, other]), jnp.stack([other, plane]))
    both = both.reshape(2, lax.axis_size("x"), lax.axis_size("tensor"), *value.shape)
    both = jnp.transpose(both, (1, 0, 2, 3, 4))
    return both.reshape(-1, value.shape[1])


def local(
    context,
    w_out,
    teacher_input,
    teacher_gain,
    layer_weights,
    teacher_head,
    student_hidden,
    student_input,
    down_weight,
    student_gain,
    student_head,
    labels,
    lengths,
):
    tok_rows = teacher_input.shape[0]
    attention = teacher_attention(context, w_out, tok_rows)
    group = lax.axis_size(GROUP)
    outer = lax.axis_size("q")
    hidden_cols = student_hidden.shape[1]
    block = hidden_cols // (group * outer)
    hidden_split = student_hidden.reshape(tok_rows, outer, group, block)
    hidden_split = jnp.transpose(hidden_split, (2, 0, 1, 3)).reshape(group, tok_rows, outer * block)
    me = lax.axis_index(GROUP)
    pieces = [hidden_split[me]]
    for k in range(1, group):
        send = lax.dynamic_index_in_dim(hidden_split, (me - k) % group, 0, keepdims=False)
        pieces.append(
            lax.ppermute(send, GROUP, perm=[(i, (i - k) % group) for i in range(group)])
        )
    hidden_mine = jnp.roll(jnp.stack(pieces), me, axis=0).reshape(group * tok_rows, -1)
    hidden_mine, attention = lax.optimization_barrier((hidden_mine, attention))
    residual = teacher_input.astype(jnp.float32)
    layer_out = norm_rows(residual + attention, teacher_gain.astype(jnp.float32), teacher_eps)[0]
    blended = (layer_weights[0] * residual + layer_weights[1] * layer_out).astype(jnp.bfloat16)
    teacher_logits = jnp.dot(blended, teacher_head, preferred_element_type=jnp.float32)
    teacher_logp = jax.nn.log_softmax(teacher_logits, axis=-1)
    teacher_prob = jnp.exp(teacher_logp)
    ffn_out = folder(student_hidden, lax.all_gather(down_weight, TOKS, axis=0, tiled=True))
    student_scale = student_gain.astype(jnp.float32)
    normed, scaled, inverse = norm_rows(
        student_input.astype(jnp.float32) + ffn_out, student_scale, student_eps
    )
    features = normed.astype(jnp.bfloat16)
    student_logits = jnp.dot(features, student_head, preferred_element_type=jnp.float32)
    student_logp = jax.nn.log_softmax(student_logits, axis=-1)
    student_prob = jnp.exp(student_logp)
    first_token = lax.axis_index(TOKS) * tok_rows
    positions = first_token + jnp.arange(tok_rows, dtype=jnp.int32)
    sentence = positions // SEQ
    matches = sentence[:, None] == jnp.arange(lengths.shape[0], dtype=jnp.int32)[None, :]
    lengths_tok = jnp.sum(jnp.where(matches, lengths[None, :], 0), axis=1)
    validity = (positions % SEQ < lengths_tok).astype(jnp.float32)
    onehot = (
        labels[:, None] == jnp.arange(teacher_logits.shape[1], dtype=jnp.int32)[None, :]
    ).astype(jnp.float32)
    token_loss = jnp.sum(
        teacher_prob * (teacher_logp - student_logp), axis=1
    ) - label_weight * jnp.sum(onehot * student_logp, axis=1)
    loss_part = jnp.sum(validity * token_loss)
    logit_grad = (
        validity[:, None]
        * ((1.0 + label_weight) * student_prob - teacher_prob - label_weight * onehot)
    ).astype(jnp.bfloat16)
    head_term = lax.dot_general(
        features, logit_grad, (((0,), (0,)), ((), ())), preferred_element_type=jnp.float32
    )
    norm_grad = (
        jnp.dot(logit_grad, student_head.T, preferred_element_type=jnp.float32) * student_scale
    )
    grad_out = (
        (
            norm_grad
            - jnp.mean(norm_grad, axis=-1, keepdims=True)
            - scaled * jnp.mean(norm_grad * scaled, axis=-1, keepdims=True)
        )
        * inverse
    ).astype(jnp.bfloat16)
    grad_out_group = group_gather(grad_out)
    grad_block = lax.dot_general(
        hidden_mine, grad_out_group, (((0,), (0,)), ((), ())), preferred_element_type=jnp.float32
    )
    grad_down = lax.psum_scatter(
        grad_block, "q", scatter_dimension=0, tiled=True
    )
    classes = head_term.shape[1]
    packed = jnp.concatenate(
        [head_term.reshape(-1), jnp.stack([loss_part, jnp.sum(validity)])]
    )
    packed = butterfly_sum(packed, ("tensor", "c", "x", "q"))
    head_total = packed[: head_term.size].reshape(-1, classes)
    return (grad_down, head_total, packed[head_term.size] / packed[head_term.size + 1])


def solution(mesh):
    dp = mesh.shape["dp"]
    tensor = mesh.shape["tensor"]
    devices = np.asarray(mesh.devices).reshape(dp // 4, 2, 2, tensor)
    fine = Mesh(devices, TOKS)
    rows = P(TOKS, None)
    return jax.shard_map(
        local,
        mesh=fine,
        in_specs=(
            P(("q", "x", "c"), "tensor"),
            P("tensor", None),
            rows,
            P(),
            P(),
            P(),
            rows,
            rows,
            rows,
            P(),
            P(),
            P(TOKS),
            P(),
        ),
        out_specs=(rows, P(), P()),
        check_vma=False,
    )
```

```python
import jax
import jax.numpy as jnp
import numpy as np
from jax import lax
from jax.sharding import Mesh
from jax.sharding import PartitionSpec as P

SEQ = 512


label_weight = 0.5
teacher_eps = 1e-05
student_eps = 1e-07

TOKS = ("q", "x", "c", "tensor")
GROUP = ("x", "c", "tensor")


def norm_rows(values, gain_vec, epsilon):
    center = values - jnp.mean(values, axis=-1, keepdims=True)
    spread = jnp.mean(center * center, axis=-1, keepdims=True)
    inverse = lax.rsqrt(spread + epsilon)
    scaled = center * inverse
    return (scaled * gain_vec, scaled, inverse)


def folder(ordered, row_piece):
    return jnp.dot(ordered, row_piece, preferred_element_type=jnp.float32)


def teacher_attention(context, w_out, tok_rows):
    tensor_size = lax.axis_size("tensor")
    partial = jnp.dot(context, w_out, preferred_element_type=jnp.float32).astype(jnp.bfloat16)
    if tensor_size != 2:
        return lax.psum_scatter(
            partial, "tensor", scatter_dimension=0, tiled=True
        ).astype(jnp.float32)
    me = lax.axis_index("tensor")
    halves = partial.reshape(2, tok_rows, partial.shape[1])
    mine = jnp.where(me == 0, halves[0], halves[1])
    theirs = jnp.where(me == 0, halves[1], halves[0])
    got = lax.ppermute(theirs, "tensor", perm=[(0, 1), (1, 0)])
    return mine.astype(jnp.float32) + got.astype(jnp.float32)


def butterfly_sum(value, axes):
    for axis in axes:
        size = lax.axis_size(axis)
        if size & (size - 1):
            value = lax.psum(value, axis)
            continue
        step = 1
        while step < size:
            value = value + lax.ppermute(
                value, axis, perm=[(i, i ^ step) for i in range(size)]
            )
            step *= 2
    return value


def group_gather(value):
    chips = ("x", "tensor")
    n = lax.axis_size(chips)
    j = lax.axis_index(chips)
    parts = [value] + [
        lax.ppermute(value, chips, perm=[(i, (i - k) % n) for i in range(n)])
        for k in range(1, n)
    ]
    plane = jnp.roll(jnp.stack(parts), j, axis=0)
    other = lax.ppermute(plane, "c", perm=[(0, 1), (1, 0)])
    low = lax.axis_index("c") == 0
    both = jnp.where(low, jnp.stack([plane, other]), jnp.stack([other, plane]))
    both = both.reshape(2, lax.axis_size("x"), lax.axis_size("tensor"), *value.shape)
    both = jnp.transpose(both, (1, 0, 2, 3, 4))
    return both.reshape(-1, value.shape[1])


def ring_gather(value, axes):
    n = lax.axis_size(axes)
    j = lax.axis_index(axes)
    parts = [value] + [
        lax.ppermute(value, axes, perm=[(i, (i - k) % n) for i in range(n)])
        for k in range(1, n)
    ]
    return jnp.roll(jnp.stack(parts), j, axis=0)


def down_weight_ffn(student_hidden, down_weight):
    along_z = ring_gather(down_weight, "q")
    plane = ring_gather(along_z, ("x", "tensor"))
    other = lax.ppermute(plane, "c", perm=[(0, 1), (1, 0)])
    core = lax.axis_index("c")
    sizes = (lax.axis_size("q"), lax.axis_size("x"), 2, lax.axis_size("tensor"))
    tok_rows = student_hidden.shape[0]
    order = student_hidden.reshape(tok_rows, *sizes, down_weight.shape[0])
    order = jnp.transpose(order, (0, 3, 2, 4, 1, 5)).reshape(tok_rows, 2, -1)
    mine_cols = lax.dynamic_index_in_dim(order, core, 1, keepdims=False)
    other_cols = lax.dynamic_index_in_dim(order, 1 - core, 1, keepdims=False)
    width = down_weight.shape[1]
    return folder(mine_cols, plane.reshape(-1, width)) + folder(
        other_cols, other.reshape(-1, width)
    )


def local(
    context,
    w_out,
    teacher_input,
    teacher_gain,
    layer_weights,
    teacher_head,
    student_hidden,
    student_input,
    down_weight,
    student_gain,
    student_head,
    labels,
    lengths,
):
    tok_rows = teacher_input.shape[0]
    attention = teacher_attention(context, w_out, tok_rows)
    group = lax.axis_size(GROUP)
    outer = lax.axis_size("q")
    hidden_cols = student_hidden.shape[1]
    block = hidden_cols // (group * outer)
    hidden_split = student_hidden.reshape(tok_rows, outer, group, block)
    hidden_split = jnp.transpose(hidden_split, (2, 0, 1, 3)).reshape(group, tok_rows, outer * block)
    me = lax.axis_index(GROUP)
    pieces = [hidden_split[me]]
    for k in range(1, group):
        send = lax.dynamic_index_in_dim(hidden_split, (me - k) % group, 0, keepdims=False)
        pieces.append(
            lax.ppermute(send, GROUP, perm=[(i, (i - k) % group) for i in range(group)])
        )
    hidden_mine = jnp.roll(jnp.stack(pieces), me, axis=0).reshape(group * tok_rows, -1)
    hidden_mine, attention = lax.optimization_barrier((hidden_mine, attention))
    residual = teacher_input.astype(jnp.float32)
    layer_out = norm_rows(residual + attention, teacher_gain.astype(jnp.float32), teacher_eps)[0]
    blended = (layer_weights[0] * residual + layer_weights[1] * layer_out).astype(jnp.bfloat16)
    teacher_logits = jnp.dot(blended, teacher_head, preferred_element_type=jnp.float32)
    teacher_logp = jax.nn.log_softmax(teacher_logits, axis=-1)
    teacher_prob = jnp.exp(teacher_logp)
    ffn_out = down_weight_ffn(student_hidden, down_weight)
    student_scale = student_gain.astype(jnp.float32)
    normed, scaled, inverse = norm_rows(
        student_input.astype(jnp.float32) + ffn_out, student_scale, student_eps
    )
    features = normed.astype(jnp.bfloat16)
    student_logits = jnp.dot(features, student_head, preferred_element_type=jnp.float32)
    student_logp = jax.nn.log_softmax(student_logits, axis=-1)
    student_prob = jnp.exp(student_logp)
    first_token = lax.axis_index(TOKS) * tok_rows
    positions = first_token + jnp.arange(tok_rows, dtype=jnp.int32)
    sentence = positions // SEQ
    matches = sentence[:, None] == jnp.arange(lengths.shape[0], dtype=jnp.int32)[None, :]
    lengths_tok = jnp.sum(jnp.where(matches, lengths[None, :], 0), axis=1)
    validity = (positions % SEQ < lengths_tok).astype(jnp.float32)
    onehot = (
        labels[:, None] == jnp.arange(teacher_logits.shape[1], dtype=jnp.int32)[None, :]
    ).astype(jnp.float32)
    token_loss = jnp.sum(
        teacher_prob * (teacher_logp - student_logp), axis=1
    ) - label_weight * jnp.sum(onehot * student_logp, axis=1)
    loss_part = jnp.sum(validity * token_loss)
    logit_grad = (
        validity[:, None]
        * ((1.0 + label_weight) * student_prob - teacher_prob - label_weight * onehot)
    ).astype(jnp.bfloat16)
    head_term = lax.dot_general(
        features, logit_grad, (((0,), (0,)), ((), ())), preferred_element_type=jnp.float32
    )
    norm_grad = (
        jnp.dot(logit_grad, student_head.T, preferred_element_type=jnp.float32) * student_scale
    )
    grad_out = (
        (
            norm_grad
            - jnp.mean(norm_grad, axis=-1, keepdims=True)
            - scaled * jnp.mean(norm_grad * scaled, axis=-1, keepdims=True)
        )
        * inverse
    ).astype(jnp.bfloat16)
    grad_out_group = group_gather(grad_out)
    grad_block = lax.dot_general(
        hidden_mine, grad_out_group, (((0,), (0,)), ((), ())), preferred_element_type=jnp.float32
    )
    grad_down = lax.psum_scatter(
        grad_block, "q", scatter_dimension=0, tiled=True
    )
    classes = head_term.shape[1]
    packed = jnp.concatenate(
        [head_term.reshape(-1), jnp.stack([loss_part, jnp.sum(validity)])]
    )
    packed = butterfly_sum(packed, ("tensor", "c", "x", "q"))
    head_total = packed[: head_term.size].reshape(-1, classes)
    return (grad_down, head_total, packed[head_term.size] / packed[head_term.size + 1])


def solution(mesh):
    dp = mesh.shape["dp"]
    tensor = mesh.shape["tensor"]
    devices = np.asarray(mesh.devices).reshape(dp // 4, 2, 2, tensor)
    fine = Mesh(devices, TOKS)
    rows = P(TOKS, None)
    return jax.shard_map(
        local,
        mesh=fine,
        in_specs=(
            P(("q", "x", "c"), "tensor"),
            P("tensor", None),
            rows,
            P(),
            P(),
            P(),
            rows,
            rows,
            rows,
            P(),
            P(),
            P(TOKS),
            P(),
        ),
        out_specs=(rows, P(), P()),
        check_vma=False,
    )
```

```python
import jax
import jax.numpy as jnp
import numpy as np
from jax import lax
from jax.sharding import Mesh
from jax.sharding import PartitionSpec as P

SEQ = 512


label_weight = 0.5
teacher_eps = 1e-05
student_eps = 1e-07

TOKS = ("q", "x", "c", "tensor")
GROUP = ("x", "c", "tensor")


def norm_rows(values, gain_vec, epsilon):
    center = values - jnp.mean(values, axis=-1, keepdims=True)
    spread = jnp.mean(center * center, axis=-1, keepdims=True)
    inverse = lax.rsqrt(spread + epsilon)
    scaled = center * inverse
    return (scaled * gain_vec, scaled, inverse)


def folder(ordered, row_piece):
    return jnp.dot(ordered, row_piece, preferred_element_type=jnp.float32)


def teacher_attention(context, w_out, tok_rows):
    tensor_size = lax.axis_size("tensor")
    partial = jnp.dot(context, w_out, preferred_element_type=jnp.float32).astype(jnp.bfloat16)
    if tensor_size != 2:
        return lax.psum_scatter(
            partial, "tensor", scatter_dimension=0, tiled=True
        ).astype(jnp.float32)
    me = lax.axis_index("tensor")
    halves = partial.reshape(2, tok_rows, partial.shape[1])
    mine = jnp.where(me == 0, halves[0], halves[1])
    theirs = jnp.where(me == 0, halves[1], halves[0])
    got = lax.ppermute(theirs, "tensor", perm=[(0, 1), (1, 0)])
    return mine.astype(jnp.float32) + got.astype(jnp.float32)


def butterfly_sum(value, axes):
    for axis in axes:
        size = lax.axis_size(axis)
        if size & (size - 1):
            value = lax.psum(value, axis)
            continue
        step = 1
        while step < size:
            value = value + lax.ppermute(
                value, axis, perm=[(i, i ^ step) for i in range(size)]
            )
            step *= 2
    return value


def group_gather(value):
    chips = ("x", "tensor")
    n = lax.axis_size(chips)
    j = lax.axis_index(chips)
    parts = [value] + [
        lax.ppermute(value, chips, perm=[(i, (i - k) % n) for i in range(n)])
        for k in range(1, n)
    ]
    plane = jnp.roll(jnp.stack(parts), j, axis=0)
    other = lax.ppermute(plane, "c", perm=[(0, 1), (1, 0)])
    low = lax.axis_index("c") == 0
    both = jnp.where(low, jnp.stack([plane, other]), jnp.stack([other, plane]))
    both = both.reshape(2, lax.axis_size("x"), lax.axis_size("tensor"), *value.shape)
    both = jnp.transpose(both, (1, 0, 2, 3, 4))
    return both.reshape(-1, value.shape[1])


def local(
    context,
    w_out,
    teacher_input,
    teacher_gain,
    layer_weights,
    teacher_head,
    student_hidden,
    student_input,
    down_weight,
    student_gain,
    student_head,
    labels,
    lengths,
):
    tok_rows = teacher_input.shape[0]
    attention = teacher_attention(context, w_out, tok_rows)
    group = lax.axis_size(GROUP)
    outer = lax.axis_size("q")
    hidden_cols = student_hidden.shape[1]
    block = hidden_cols // (group * outer)
    hidden_split = student_hidden.reshape(tok_rows, outer, group, block)
    hidden_split = jnp.transpose(hidden_split, (2, 0, 1, 3)).reshape(group, tok_rows, outer * block)
    me = lax.axis_index(GROUP)
    pieces = [hidden_split[me]]
    for k in range(1, group):
        send = lax.dynamic_index_in_dim(hidden_split, (me - k) % group, 0, keepdims=False)
        pieces.append(
            lax.ppermute(send, GROUP, perm=[(i, (i - k) % group) for i in range(group)])
        )
    hidden_mine = jnp.roll(jnp.stack(pieces), me, axis=0).reshape(group * tok_rows, -1)
    hidden_mine, attention = lax.optimization_barrier((hidden_mine, attention))
    residual = teacher_input.astype(jnp.float32)
    layer_out = norm_rows(residual + attention, teacher_gain.astype(jnp.float32), teacher_eps)[0]
    blended = (layer_weights[0] * residual + layer_weights[1] * layer_out).astype(jnp.bfloat16)
    teacher_logits = jnp.dot(blended, teacher_head, preferred_element_type=jnp.float32)
    teacher_logp = jax.nn.log_softmax(teacher_logits, axis=-1)
    teacher_prob = jnp.exp(teacher_logp)
    ffn_out = folder(student_hidden, lax.all_gather(down_weight, TOKS, axis=0, tiled=True))
    student_scale = student_gain.astype(jnp.float32)
    normed, scaled, inverse = norm_rows(
        student_input.astype(jnp.float32) + ffn_out, student_scale, student_eps
    )
    features = normed.astype(jnp.bfloat16)
    student_logits = jnp.dot(features, student_head, preferred_element_type=jnp.float32)
    student_logp = jax.nn.log_softmax(student_logits, axis=-1)
    student_prob = jnp.exp(student_logp)
    first_token = lax.axis_index(TOKS) * tok_rows
    positions = first_token + jnp.arange(tok_rows, dtype=jnp.int32)
    sentence = positions // SEQ
    matches = sentence[:, None] == jnp.arange(lengths.shape[0], dtype=jnp.int32)[None, :]
    lengths_tok = jnp.sum(jnp.where(matches, lengths[None, :], 0), axis=1)
    validity = (positions % SEQ < lengths_tok).astype(jnp.float32)
    onehot = (
        labels[:, None] == jnp.arange(teacher_logits.shape[1], dtype=jnp.int32)[None, :]
    ).astype(jnp.float32)
    token_loss = jnp.sum(
        teacher_prob * (teacher_logp - student_logp), axis=1
    ) - label_weight * jnp.sum(onehot * student_logp, axis=1)
    loss_part = jnp.sum(validity * token_loss)
    logit_grad = (
        validity[:, None]
        * ((1.0 + label_weight) * student_prob - teacher_prob - label_weight * onehot)
    ).astype(jnp.bfloat16)
    head_term = lax.dot_general(
        features, logit_grad, (((0,), (0,)), ((), ())), preferred_element_type=jnp.float32
    )
    norm_grad = (
        jnp.dot(logit_grad, student_head.T, preferred_element_type=jnp.float32) * student_scale
    )
    grad_out = (
        (
            norm_grad
            - jnp.mean(norm_grad, axis=-1, keepdims=True)
            - scaled * jnp.mean(norm_grad * scaled, axis=-1, keepdims=True)
        )
        * inverse
    ).astype(jnp.bfloat16)
    grad_out_group = group_gather(grad_out)
    grad_block = lax.dot_general(
        hidden_mine, grad_out_group, (((0,), (0,)), ((), ())), preferred_element_type=jnp.float32
    )
    outer_me = lax.axis_index("q")
    row_blocks = grad_block.reshape(outer, -1, grad_block.shape[1])
    grad_down = lax.dynamic_index_in_dim(row_blocks, outer_me, 0, keepdims=False)
    for k in range(1, outer):
        send = lax.dynamic_index_in_dim(row_blocks, (outer_me - k) % outer, 0, keepdims=False)
        grad_down = grad_down + lax.ppermute(
            send, "q", perm=[(i, (i - k) % outer) for i in range(outer)]
        )
    classes = head_term.shape[1]
    packed = jnp.concatenate(
        [head_term.reshape(-1), jnp.stack([loss_part, jnp.sum(validity)])]
    )
    packed = butterfly_sum(packed, ("tensor", "c", "x", "q"))
    head_total = packed[: head_term.size].reshape(-1, classes)
    return (grad_down, head_total, packed[head_term.size] / packed[head_term.size + 1])


def solution(mesh):
    dp = mesh.shape["dp"]
    tensor = mesh.shape["tensor"]
    devices = np.asarray(mesh.devices).reshape(dp // 4, 2, 2, tensor)
    fine = Mesh(devices, TOKS)
    rows = P(TOKS, None)
    return jax.shard_map(
        local,
        mesh=fine,
        in_specs=(
            P(("q", "x", "c"), "tensor"),
            P("tensor", None),
            rows,
            P(),
            P(),
            P(),
            rows,
            rows,
            rows,
            P(),
            P(),
            P(TOKS),
            P(),
        ),
        out_specs=(rows, P(), P()),
        check_vma=False,
    )
```

```python
import jax
import jax.numpy as jnp
import numpy as np
from jax import lax
from jax.sharding import Mesh
from jax.sharding import PartitionSpec as P

SEQ = 512


label_weight = 0.5
teacher_eps = 1e-05
student_eps = 1e-07

TOKS = ("q", "x", "c", "tensor")
GROUP = ("x", "c", "tensor")


def norm_rows(values, gain_vec, epsilon):
    center = values - jnp.mean(values, axis=-1, keepdims=True)
    spread = jnp.mean(center * center, axis=-1, keepdims=True)
    inverse = lax.rsqrt(spread + epsilon)
    scaled = center * inverse
    return (scaled * gain_vec, scaled, inverse)


def folder(ordered, row_piece):
    return jnp.dot(ordered, row_piece, preferred_element_type=jnp.float32)


def teacher_attention(context, w_out, tok_rows):
    tensor_size = lax.axis_size("tensor")
    partial = jnp.dot(context, w_out, preferred_element_type=jnp.float32).astype(jnp.bfloat16)
    if tensor_size != 2:
        return lax.psum_scatter(
            partial, "tensor", scatter_dimension=0, tiled=True
        ).astype(jnp.float32)
    me = lax.axis_index("tensor")
    halves = partial.reshape(2, tok_rows, partial.shape[1])
    mine = jnp.where(me == 0, halves[0], halves[1])
    theirs = jnp.where(me == 0, halves[1], halves[0])
    got = lax.ppermute(theirs, "tensor", perm=[(0, 1), (1, 0)])
    return mine.astype(jnp.float32) + got.astype(jnp.float32)


def butterfly_sum(value, axes):
    for axis in axes:
        size = lax.axis_size(axis)
        if size & (size - 1):
            value = lax.psum(value, axis)
            continue
        step = 1
        while step < size:
            value = value + lax.ppermute(
                value, axis, perm=[(i, i ^ step) for i in range(size)]
            )
            step *= 2
    return value


def group_gather(value):
    chips = ("x", "tensor")
    n = lax.axis_size(chips)
    j = lax.axis_index(chips)
    parts = [value] + [
        lax.ppermute(value, chips, perm=[(i, (i - k) % n) for i in range(n)])
        for k in range(1, n)
    ]
    plane = jnp.roll(jnp.stack(parts), j, axis=0)
    other = lax.ppermute(plane, "c", perm=[(0, 1), (1, 0)])
    low = lax.axis_index("c") == 0
    both = jnp.where(low, jnp.stack([plane, other]), jnp.stack([other, plane]))
    both = both.reshape(2, lax.axis_size("x"), lax.axis_size("tensor"), *value.shape)
    both = jnp.transpose(both, (1, 0, 2, 3, 4))
    return both.reshape(-1, value.shape[1])


def local(
    context,
    w_out,
    teacher_input,
    teacher_gain,
    layer_weights,
    teacher_head,
    student_hidden,
    student_input,
    down_weight,
    student_gain,
    student_head,
    labels,
    lengths,
):
    tok_rows = teacher_input.shape[0]
    attention = teacher_attention(context, w_out, tok_rows)
    group = lax.axis_size(GROUP)
    outer = lax.axis_size("q")
    hidden_cols = student_hidden.shape[1]
    block = hidden_cols // (group * outer)
    hidden_split = student_hidden.reshape(tok_rows, outer, group, block)
    hidden_split = jnp.transpose(hidden_split, (2, 0, 1, 3)).reshape(group, tok_rows, outer * block)
    me = lax.axis_index(GROUP)
    pieces = [hidden_split[me]]
    for k in range(1, group):
        send = lax.dynamic_index_in_dim(hidden_split, (me - k) % group, 0, keepdims=False)
        pieces.append(
            lax.ppermute(send, GROUP, perm=[(i, (i - k) % group) for i in range(group)])
        )
    hidden_mine = jnp.roll(jnp.stack(pieces), me, axis=0).reshape(group * tok_rows, -1)
    hidden_mine, attention = lax.optimization_barrier((hidden_mine, attention))
    residual = teacher_input.astype(jnp.float32)
    layer_out = norm_rows(residual + attention, teacher_gain.astype(jnp.float32), teacher_eps)[0]
    blended = (layer_weights[0] * residual + layer_weights[1] * layer_out).astype(jnp.bfloat16)
    teacher_logits = jnp.dot(blended, teacher_head, preferred_element_type=jnp.float32)
    teacher_logp = jax.nn.log_softmax(teacher_logits, axis=-1)
    teacher_prob = jnp.exp(teacher_logp)
    ffn_out = folder(student_hidden, lax.all_gather(down_weight, TOKS, axis=0, tiled=True))
    student_scale = student_gain.astype(jnp.float32)
    normed, scaled, inverse = norm_rows(
        student_input.astype(jnp.float32) + ffn_out, student_scale, student_eps
    )
    features = normed.astype(jnp.bfloat16)
    student_logits = jnp.dot(features, student_head, preferred_element_type=jnp.float32)
    student_logp = jax.nn.log_softmax(student_logits, axis=-1)
    student_prob = jnp.exp(student_logp)
    first_token = lax.axis_index(TOKS) * tok_rows
    positions = first_token + jnp.arange(tok_rows, dtype=jnp.int32)
    sentence = positions // SEQ
    matches = sentence[:, None] == jnp.arange(lengths.shape[0], dtype=jnp.int32)[None, :]
    lengths_tok = jnp.sum(jnp.where(matches, lengths[None, :], 0), axis=1)
    validity = (positions % SEQ < lengths_tok).astype(jnp.float32)
    onehot = (
        labels[:, None] == jnp.arange(teacher_logits.shape[1], dtype=jnp.int32)[None, :]
    ).astype(jnp.float32)
    token_loss = jnp.sum(
        teacher_prob * (teacher_logp - student_logp), axis=1
    ) - label_weight * jnp.sum(onehot * student_logp, axis=1)
    loss_part = jnp.sum(validity * token_loss)
    logit_grad = (
        validity[:, None]
        * ((1.0 + label_weight) * student_prob - teacher_prob - label_weight * onehot)
    ).astype(jnp.bfloat16)
    head_term = lax.dot_general(
        features, logit_grad, (((0,), (0,)), ((), ())), preferred_element_type=jnp.float32
    )
    norm_grad = (
        jnp.dot(logit_grad, student_head.T, preferred_element_type=jnp.float32) * student_scale
    )
    grad_out = (
        (
            norm_grad
            - jnp.mean(norm_grad, axis=-1, keepdims=True)
            - scaled * jnp.mean(norm_grad * scaled, axis=-1, keepdims=True)
        )
        * inverse
    ).astype(jnp.bfloat16)
    half = grad_out.shape[1] // 2
    grad_down = jnp.concatenate(
        [
            lax.psum_scatter(
                lax.dot_general(
                    hidden_mine,
                    group_gather(cols),
                    (((0,), (0,)), ((), ())),
                    preferred_element_type=jnp.float32,
                ),
                "q",
                scatter_dimension=0,
                tiled=True,
            )
            for cols in (grad_out[:, :half], grad_out[:, half:])
        ],
        axis=1,
    )
    classes = head_term.shape[1]
    packed = jnp.concatenate(
        [head_term.reshape(-1), jnp.stack([loss_part, jnp.sum(validity)])]
    )
    packed = butterfly_sum(packed, ("tensor", "c", "x", "q"))
    head_total = packed[: head_term.size].reshape(-1, classes)
    return (grad_down, head_total, packed[head_term.size] / packed[head_term.size + 1])


def solution(mesh):
    dp = mesh.shape["dp"]
    tensor = mesh.shape["tensor"]
    devices = np.asarray(mesh.devices).reshape(dp // 4, 2, 2, tensor)
    fine = Mesh(devices, TOKS)
    rows = P(TOKS, None)
    return jax.shard_map(
        local,
        mesh=fine,
        in_specs=(
            P(("q", "x", "c"), "tensor"),
            P("tensor", None),
            rows,
            P(),
            P(),
            P(),
            rows,
            rows,
            rows,
            P(),
            P(),
            P(TOKS),
            P(),
        ),
        out_specs=(rows, P(), P()),
        check_vma=False,
    )
```

```python
import jax
import jax.numpy as jnp
import numpy as np
from jax import lax
from jax.sharding import Mesh
from jax.sharding import PartitionSpec as P

SEQ = 512


label_weight = 0.5
teacher_eps = 1e-05
student_eps = 1e-07

TOKS = ("q", "x", "c", "tensor")
GROUP = ("x", "c", "tensor")


def norm_rows(values, gain_vec, epsilon):
    center = values - jnp.mean(values, axis=-1, keepdims=True)
    spread = jnp.mean(center * center, axis=-1, keepdims=True)
    inverse = lax.rsqrt(spread + epsilon)
    scaled = center * inverse
    return (scaled * gain_vec, scaled, inverse)


def folder(ordered, row_piece):
    return jnp.dot(ordered, row_piece, preferred_element_type=jnp.float32)


def teacher_attention(context, w_out, tok_rows):
    tensor_size = lax.axis_size("tensor")
    partial = jnp.dot(context, w_out, preferred_element_type=jnp.float32).astype(jnp.bfloat16)
    if tensor_size != 2:
        return lax.psum_scatter(
            partial, "tensor", scatter_dimension=0, tiled=True
        ).astype(jnp.float32)
    me = lax.axis_index("tensor")
    halves = partial.reshape(2, tok_rows, partial.shape[1])
    mine = jnp.where(me == 0, halves[0], halves[1])
    theirs = jnp.where(me == 0, halves[1], halves[0])
    got = lax.ppermute(theirs, "tensor", perm=[(0, 1), (1, 0)])
    return mine.astype(jnp.float32) + got.astype(jnp.float32)


def butterfly_sum(value, axes):
    for axis in axes:
        size = lax.axis_size(axis)
        if size & (size - 1):
            value = lax.psum(value, axis)
            continue
        step = 1
        while step < size:
            value = value + lax.ppermute(
                value, axis, perm=[(i, i ^ step) for i in range(size)]
            )
            step *= 2
    return value


def group_gather(value):
    chips = ("x", "tensor")
    n = lax.axis_size(chips)
    j = lax.axis_index(chips)
    parts = [value] + [
        lax.ppermute(value, chips, perm=[(i, (i - k) % n) for i in range(n)])
        for k in range(1, n)
    ]
    plane = jnp.roll(jnp.stack(parts), j, axis=0)
    other = lax.ppermute(plane, "c", perm=[(0, 1), (1, 0)])
    low = lax.axis_index("c") == 0
    both = jnp.where(low, jnp.stack([plane, other]), jnp.stack([other, plane]))
    both = both.reshape(2, lax.axis_size("x"), lax.axis_size("tensor"), *value.shape)
    both = jnp.transpose(both, (1, 0, 2, 3, 4))
    return both.reshape(-1, value.shape[1])


def ring_gather(value, axes):
    n = lax.axis_size(axes)
    j = lax.axis_index(axes)
    parts = [value] + [
        lax.ppermute(value, axes, perm=[(i, (i - k) % n) for i in range(n)])
        for k in range(1, n)
    ]
    return jnp.roll(jnp.stack(parts), j, axis=0)


def ring_scatter_sum(blocks, axes):
    n = lax.axis_size(axes)
    j = lax.axis_index(axes)
    total = lax.dynamic_index_in_dim(blocks, j, 0, keepdims=False)
    for k in range(1, n):
        send = lax.dynamic_index_in_dim(blocks, (j - k) % n, 0, keepdims=False)
        total = total + lax.ppermute(send, axes, perm=[(i, (i - k) % n) for i in range(n)])
    return total


def local(
    context,
    w_out,
    teacher_input,
    teacher_gain,
    layer_weights,
    teacher_head,
    student_hidden,
    student_input,
    down_weight,
    student_gain,
    student_head,
    labels,
    lengths,
):
    tok_rows = teacher_input.shape[0]
    attention = teacher_attention(context, w_out, tok_rows)
    group = lax.axis_size(GROUP)
    outer = lax.axis_size("q")
    hidden_cols = student_hidden.shape[1]
    block = hidden_cols // (group * outer)
    hidden_split = student_hidden.reshape(tok_rows, outer, group, block)
    hidden_split = jnp.transpose(hidden_split, (2, 0, 1, 3)).reshape(group, tok_rows, outer * block)
    me = lax.axis_index(GROUP)
    pieces = [hidden_split[me]]
    for k in range(1, group):
        send = lax.dynamic_index_in_dim(hidden_split, (me - k) % group, 0, keepdims=False)
        pieces.append(
            lax.ppermute(send, GROUP, perm=[(i, (i - k) % group) for i in range(group)])
        )
    hidden_mine = jnp.roll(jnp.stack(pieces), me, axis=0).reshape(group * tok_rows, -1)
    hidden_mine, attention = lax.optimization_barrier((hidden_mine, attention))
    strided_rows = ring_gather(down_weight, "q").reshape(-1, down_weight.shape[1])
    ffn_terms = folder(hidden_mine, strided_rows).reshape(group, tok_rows, -1)
    ffn_out = ring_scatter_sum(ffn_terms, GROUP)
    residual = teacher_input.astype(jnp.float32)
    layer_out = norm_rows(residual + attention, teacher_gain.astype(jnp.float32), teacher_eps)[0]
    blended = (layer_weights[0] * residual + layer_weights[1] * layer_out).astype(jnp.bfloat16)
    teacher_logits = jnp.dot(blended, teacher_head, preferred_element_type=jnp.float32)
    teacher_logp = jax.nn.log_softmax(teacher_logits, axis=-1)
    teacher_prob = jnp.exp(teacher_logp)
    student_scale = student_gain.astype(jnp.float32)
    normed, scaled, inverse = norm_rows(
        student_input.astype(jnp.float32) + ffn_out, student_scale, student_eps
    )
    features = normed.astype(jnp.bfloat16)
    student_logits = jnp.dot(features, student_head, preferred_element_type=jnp.float32)
    student_logp = jax.nn.log_softmax(student_logits, axis=-1)
    student_prob = jnp.exp(student_logp)
    first_token = lax.axis_index(TOKS) * tok_rows
    positions = first_token + jnp.arange(tok_rows, dtype=jnp.int32)
    sentence = positions // SEQ
    matches = sentence[:, None] == jnp.arange(lengths.shape[0], dtype=jnp.int32)[None, :]
    lengths_tok = jnp.sum(jnp.where(matches, lengths[None, :], 0), axis=1)
    validity = (positions % SEQ < lengths_tok).astype(jnp.float32)
    onehot = (
        labels[:, None] == jnp.arange(teacher_logits.shape[1], dtype=jnp.int32)[None, :]
    ).astype(jnp.float32)
    token_loss = jnp.sum(
        teacher_prob * (teacher_logp - student_logp), axis=1
    ) - label_weight * jnp.sum(onehot * student_logp, axis=1)
    loss_part = jnp.sum(validity * token_loss)
    logit_grad = (
        validity[:, None]
        * ((1.0 + label_weight) * student_prob - teacher_prob - label_weight * onehot)
    ).astype(jnp.bfloat16)
    head_term = lax.dot_general(
        features, logit_grad, (((0,), (0,)), ((), ())), preferred_element_type=jnp.float32
    )
    norm_grad = (
        jnp.dot(logit_grad, student_head.T, preferred_element_type=jnp.float32) * student_scale
    )
    grad_out = (
        (
            norm_grad
            - jnp.mean(norm_grad, axis=-1, keepdims=True)
            - scaled * jnp.mean(norm_grad * scaled, axis=-1, keepdims=True)
        )
        * inverse
    ).astype(jnp.bfloat16)
    grad_out_group = group_gather(grad_out)
    grad_block = lax.dot_general(
        hidden_mine, grad_out_group, (((0,), (0,)), ((), ())), preferred_element_type=jnp.float32
    )
    grad_down = lax.psum_scatter(
        grad_block, "q", scatter_dimension=0, tiled=True
    )
    classes = head_term.shape[1]
    packed = jnp.concatenate(
        [head_term.reshape(-1), jnp.stack([loss_part, jnp.sum(validity)])]
    )
    packed = butterfly_sum(packed, ("tensor", "c", "x", "q"))
    head_total = packed[: head_term.size].reshape(-1, classes)
    return (grad_down, head_total, packed[head_term.size] / packed[head_term.size + 1])


def solution(mesh):
    dp = mesh.shape["dp"]
    tensor = mesh.shape["tensor"]
    devices = np.asarray(mesh.devices).reshape(dp // 4, 2, 2, tensor)
    fine = Mesh(devices, TOKS)
    rows = P(TOKS, None)
    return jax.shard_map(
        local,
        mesh=fine,
        in_specs=(
            P(("q", "x", "c"), "tensor"),
            P("tensor", None),
            rows,
            P(),
            P(),
            P(),
            rows,
            rows,
            rows,
            P(),
            P(),
            P(TOKS),
            P(),
        ),
        out_specs=(rows, P(), P()),
        check_vma=False,
    )
```

```python
import jax
import jax.numpy as jnp
import numpy as np
from jax import lax
from jax.sharding import Mesh
from jax.sharding import PartitionSpec as P

SEQ = 512


label_weight = 0.5
teacher_eps = 1e-05
student_eps = 1e-07

TOKS = ("q", "x", "c", "tensor")
GROUP = ("x", "c", "tensor")


def norm_rows(values, gain_vec, epsilon):
    center = values - jnp.mean(values, axis=-1, keepdims=True)
    spread = jnp.mean(center * center, axis=-1, keepdims=True)
    inverse = lax.rsqrt(spread + epsilon)
    scaled = center * inverse
    return (scaled * gain_vec, scaled, inverse)


def folder(ordered, row_piece):
    return jnp.dot(ordered, row_piece, preferred_element_type=jnp.float32)


def teacher_attention(context, w_out, tok_rows):
    tensor_size = lax.axis_size("tensor")
    partial = jnp.dot(context, w_out, preferred_element_type=jnp.float32).astype(jnp.bfloat16)
    if tensor_size != 2:
        return lax.psum_scatter(
            partial, "tensor", scatter_dimension=0, tiled=True
        ).astype(jnp.float32)
    me = lax.axis_index("tensor")
    halves = partial.reshape(2, tok_rows, partial.shape[1])
    mine = jnp.where(me == 0, halves[0], halves[1])
    theirs = jnp.where(me == 0, halves[1], halves[0])
    got = lax.ppermute(theirs, "tensor", perm=[(0, 1), (1, 0)])
    return mine.astype(jnp.float32) + got.astype(jnp.float32)


def butterfly_sum(value, axes):
    for axis in axes:
        size = lax.axis_size(axis)
        if size & (size - 1):
            value = lax.psum(value, axis)
            continue
        step = 1
        while step < size:
            value = value + lax.ppermute(
                value, axis, perm=[(i, i ^ step) for i in range(size)]
            )
            step *= 2
    return value


def group_gather(value):
    chips = ("x", "tensor")
    n = lax.axis_size(chips)
    j = lax.axis_index(chips)
    parts = [value] + [
        lax.ppermute(value, chips, perm=[(i, (i - k) % n) for i in range(n)])
        for k in range(1, n)
    ]
    plane = jnp.roll(jnp.stack(parts), j, axis=0)
    other = lax.ppermute(plane, "c", perm=[(0, 1), (1, 0)])
    low = lax.axis_index("c") == 0
    both = jnp.where(low, jnp.stack([plane, other]), jnp.stack([other, plane]))
    both = both.reshape(2, lax.axis_size("x"), lax.axis_size("tensor"), *value.shape)
    both = jnp.transpose(both, (1, 0, 2, 3, 4))
    return both.reshape(-1, value.shape[1])


def local(
    context,
    w_out,
    teacher_input,
    teacher_gain,
    layer_weights,
    teacher_head,
    student_hidden,
    student_input,
    down_weight,
    student_gain,
    student_head,
    labels,
    lengths,
):
    tok_rows = teacher_input.shape[0]
    attention = teacher_attention(context, w_out, tok_rows)
    group = lax.axis_size(GROUP)
    outer = lax.axis_size("q")
    hidden_cols = student_hidden.shape[1]
    block = hidden_cols // (group * outer)
    hidden_split = student_hidden.reshape(tok_rows, outer, group, block)
    hidden_split = jnp.transpose(hidden_split, (2, 0, 1, 3)).reshape(group, tok_rows, outer * block)
    me = lax.axis_index(GROUP)
    pieces = [hidden_split[me]]
    for k in range(1, group):
        send = lax.dynamic_index_in_dim(hidden_split, (me - k) % group, 0, keepdims=False)
        pieces.append(
            lax.ppermute(send, GROUP, perm=[(i, (i - k) % group) for i in range(group)])
        )
    hidden_mine = jnp.roll(jnp.stack(pieces), me, axis=0).reshape(group * tok_rows, -1)
    hidden_mine, attention = lax.optimization_barrier((hidden_mine, attention))
    residual = teacher_input.astype(jnp.float32)
    layer_out = norm_rows(residual + attention, teacher_gain.astype(jnp.float32), teacher_eps)[0]
    blended = (layer_weights[0] * residual + layer_weights[1] * layer_out).astype(jnp.bfloat16)
    teacher_logits = jnp.dot(blended, teacher_head, preferred_element_type=jnp.float32)
    teacher_logp = jax.nn.log_softmax(teacher_logits, axis=-1)
    teacher_prob = jnp.exp(teacher_logp)
    gathered = lax.all_gather(down_weight, TOKS[::-1], axis=0, tiled=True)
    sizes = tuple(lax.axis_size(a) for a in TOKS)
    by_block = student_hidden.reshape(tok_rows, *sizes, down_weight.shape[0])
    by_block = jnp.transpose(by_block, (0, 4, 3, 2, 1, 5)).reshape(tok_rows, -1)
    ffn_out = folder(by_block, gathered)
    student_scale = student_gain.astype(jnp.float32)
    normed, scaled, inverse = norm_rows(
        student_input.astype(jnp.float32) + ffn_out, student_scale, student_eps
    )
    features = normed.astype(jnp.bfloat16)
    student_logits = jnp.dot(features, student_head, preferred_element_type=jnp.float32)
    student_logp = jax.nn.log_softmax(student_logits, axis=-1)
    student_prob = jnp.exp(student_logp)
    first_token = lax.axis_index(TOKS) * tok_rows
    positions = first_token + jnp.arange(tok_rows, dtype=jnp.int32)
    sentence = positions // SEQ
    matches = sentence[:, None] == jnp.arange(lengths.shape[0], dtype=jnp.int32)[None, :]
    lengths_tok = jnp.sum(jnp.where(matches, lengths[None, :], 0), axis=1)
    validity = (positions % SEQ < lengths_tok).astype(jnp.float32)
    onehot = (
        labels[:, None] == jnp.arange(teacher_logits.shape[1], dtype=jnp.int32)[None, :]
    ).astype(jnp.float32)
    token_loss = jnp.sum(
        teacher_prob * (teacher_logp - student_logp), axis=1
    ) - label_weight * jnp.sum(onehot * student_logp, axis=1)
    loss_part = jnp.sum(validity * token_loss)
    logit_grad = (
        validity[:, None]
        * ((1.0 + label_weight) * student_prob - teacher_prob - label_weight * onehot)
    ).astype(jnp.bfloat16)
    head_term = lax.dot_general(
        features, logit_grad, (((0,), (0,)), ((), ())), preferred_element_type=jnp.float32
    )
    norm_grad = (
        jnp.dot(logit_grad, student_head.T, preferred_element_type=jnp.float32) * student_scale
    )
    grad_out = (
        (
            norm_grad
            - jnp.mean(norm_grad, axis=-1, keepdims=True)
            - scaled * jnp.mean(norm_grad * scaled, axis=-1, keepdims=True)
        )
        * inverse
    ).astype(jnp.bfloat16)
    grad_out_group = group_gather(grad_out)
    grad_block = lax.dot_general(
        hidden_mine, grad_out_group, (((0,), (0,)), ((), ())), preferred_element_type=jnp.float32
    )
    grad_down = lax.psum_scatter(
        grad_block, "q", scatter_dimension=0, tiled=True
    )
    classes = head_term.shape[1]
    packed = jnp.concatenate(
        [head_term.reshape(-1), jnp.stack([loss_part, jnp.sum(validity)])]
    )
    packed = butterfly_sum(packed, ("tensor", "c", "x", "q"))
    head_total = packed[: head_term.size].reshape(-1, classes)
    return (grad_down, head_total, packed[head_term.size] / packed[head_term.size + 1])


def solution(mesh):
    dp = mesh.shape["dp"]
    tensor = mesh.shape["tensor"]
    devices = np.asarray(mesh.devices).reshape(dp // 4, 2, 2, tensor)
    fine = Mesh(devices, TOKS)
    rows = P(TOKS, None)
    return jax.shard_map(
        local,
        mesh=fine,
        in_specs=(
            P(("q", "x", "c"), "tensor"),
            P("tensor", None),
            rows,
            P(),
            P(),
            P(),
            rows,
            rows,
            rows,
            P(),
            P(),
            P(TOKS),
            P(),
        ),
        out_specs=(rows, P(), P()),
        check_vma=False,
    )
```

```python
import jax
import jax.numpy as jnp
import numpy as np
from jax import lax
from jax.sharding import Mesh
from jax.sharding import PartitionSpec as P

SEQ = 512


label_weight = 0.5
teacher_eps = 1e-05
student_eps = 1e-07

TOKS = ("q", "x", "c", "tensor")
GROUP = ("x", "c", "tensor")


def norm_rows(values, gain_vec, epsilon):
    center = values - jnp.mean(values, axis=-1, keepdims=True)
    spread = jnp.mean(center * center, axis=-1, keepdims=True)
    inverse = lax.rsqrt(spread + epsilon)
    scaled = center * inverse
    return (scaled * gain_vec, scaled, inverse)


def folder(ordered, row_piece):
    return jnp.dot(ordered, row_piece, preferred_element_type=jnp.float32)


def teacher_attention(context, w_out, tok_rows):
    tensor_size = lax.axis_size("tensor")
    partial = jnp.dot(context, w_out, preferred_element_type=jnp.float32).astype(jnp.bfloat16)
    if tensor_size != 2:
        return lax.psum_scatter(
            partial, "tensor", scatter_dimension=0, tiled=True
        ).astype(jnp.float32)
    me = lax.axis_index("tensor")
    halves = partial.reshape(2, tok_rows, partial.shape[1])
    mine = jnp.where(me == 0, halves[0], halves[1])
    theirs = jnp.where(me == 0, halves[1], halves[0])
    got = lax.ppermute(theirs, "tensor", perm=[(0, 1), (1, 0)])
    return mine.astype(jnp.float32) + got.astype(jnp.float32)


def butterfly_sum(value, axes):
    for axis in axes:
        size = lax.axis_size(axis)
        if size & (size - 1):
            value = lax.psum(value, axis)
            continue
        step = 1
        while step < size:
            value = value + lax.ppermute(
                value, axis, perm=[(i, i ^ step) for i in range(size)]
            )
            step *= 2
    return value


def group_gather(value):
    chips = ("x", "tensor")
    n = lax.axis_size(chips)
    parts = [value] + [
        lax.ppermute(value, chips, perm=[(i, (i - k) % n) for i in range(n)])
        for k in range(1, n)
    ]
    plane = jnp.concatenate(parts, axis=0)
    other = lax.ppermute(plane, "c", perm=[(0, 1), (1, 0)])
    return jnp.concatenate([plane, other], axis=0)


def group_order():
    chips = ("x", "tensor")
    n = lax.axis_size(chips)
    tensor = lax.axis_size("tensor")
    core = lax.axis_index("c")
    chip = (lax.axis_index(chips) + jnp.arange(n, dtype=jnp.int32)) % n
    x, t = chip // tensor, chip % tensor
    return jnp.concatenate([(x * 2 + core) * tensor + t, (x * 2 + 1 - core) * tensor + t])


def local(
    context,
    w_out,
    teacher_input,
    teacher_gain,
    layer_weights,
    teacher_head,
    student_hidden,
    student_input,
    down_weight,
    student_gain,
    student_head,
    labels,
    lengths,
):
    tok_rows = teacher_input.shape[0]
    attention = teacher_attention(context, w_out, tok_rows)
    group = lax.axis_size(GROUP)
    outer = lax.axis_size("q")
    hidden_cols = student_hidden.shape[1]
    block = hidden_cols // (group * outer)
    hidden_split = student_hidden.reshape(tok_rows, outer, group, block)
    hidden_split = jnp.transpose(hidden_split, (2, 0, 1, 3)).reshape(group, tok_rows, outer * block)
    me = lax.axis_index(GROUP)
    pieces = [hidden_split[me]]
    for k in range(1, group):
        send = lax.dynamic_index_in_dim(hidden_split, (me - k) % group, 0, keepdims=False)
        pieces.append(
            lax.ppermute(send, GROUP, perm=[(i, (i - k) % group) for i in range(group)])
        )
    hidden_mine = jnp.take(jnp.roll(jnp.stack(pieces), me, axis=0), group_order(), axis=0)
    hidden_mine = hidden_mine.reshape(group * tok_rows, -1)
    hidden_mine, attention = lax.optimization_barrier((hidden_mine, attention))
    residual = teacher_input.astype(jnp.float32)
    layer_out = norm_rows(residual + attention, teacher_gain.astype(jnp.float32), teacher_eps)[0]
    blended = (layer_weights[0] * residual + layer_weights[1] * layer_out).astype(jnp.bfloat16)
    teacher_logits = jnp.dot(blended, teacher_head, preferred_element_type=jnp.float32)
    teacher_logp = jax.nn.log_softmax(teacher_logits, axis=-1)
    teacher_prob = jnp.exp(teacher_logp)
    ffn_out = folder(student_hidden, lax.all_gather(down_weight, TOKS, axis=0, tiled=True))
    student_scale = student_gain.astype(jnp.float32)
    normed, scaled, inverse = norm_rows(
        student_input.astype(jnp.float32) + ffn_out, student_scale, student_eps
    )
    features = normed.astype(jnp.bfloat16)
    student_logits = jnp.dot(features, student_head, preferred_element_type=jnp.float32)
    student_logp = jax.nn.log_softmax(student_logits, axis=-1)
    student_prob = jnp.exp(student_logp)
    first_token = lax.axis_index(TOKS) * tok_rows
    positions = first_token + jnp.arange(tok_rows, dtype=jnp.int32)
    sentence = positions // SEQ
    matches = sentence[:, None] == jnp.arange(lengths.shape[0], dtype=jnp.int32)[None, :]
    lengths_tok = jnp.sum(jnp.where(matches, lengths[None, :], 0), axis=1)
    validity = (positions % SEQ < lengths_tok).astype(jnp.float32)
    onehot = (
        labels[:, None] == jnp.arange(teacher_logits.shape[1], dtype=jnp.int32)[None, :]
    ).astype(jnp.float32)
    token_loss = jnp.sum(
        teacher_prob * (teacher_logp - student_logp), axis=1
    ) - label_weight * jnp.sum(onehot * student_logp, axis=1)
    loss_part = jnp.sum(validity * token_loss)
    logit_grad = (
        validity[:, None]
        * ((1.0 + label_weight) * student_prob - teacher_prob - label_weight * onehot)
    ).astype(jnp.bfloat16)
    head_term = lax.dot_general(
        features, logit_grad, (((0,), (0,)), ((), ())), preferred_element_type=jnp.float32
    )
    norm_grad = (
        jnp.dot(logit_grad, student_head.T, preferred_element_type=jnp.float32) * student_scale
    )
    grad_out = (
        (
            norm_grad
            - jnp.mean(norm_grad, axis=-1, keepdims=True)
            - scaled * jnp.mean(norm_grad * scaled, axis=-1, keepdims=True)
        )
        * inverse
    ).astype(jnp.bfloat16)
    grad_out_group = group_gather(grad_out)
    grad_block = lax.dot_general(
        hidden_mine, grad_out_group, (((0,), (0,)), ((), ())), preferred_element_type=jnp.float32
    )
    grad_down = lax.psum_scatter(
        grad_block, "q", scatter_dimension=0, tiled=True
    )
    classes = head_term.shape[1]
    packed = jnp.concatenate(
        [head_term.reshape(-1), jnp.stack([loss_part, jnp.sum(validity)])]
    )
    packed = butterfly_sum(packed, ("tensor", "c", "x", "q"))
    head_total = packed[: head_term.size].reshape(-1, classes)
    return (grad_down, head_total, packed[head_term.size] / packed[head_term.size + 1])


def solution(mesh):
    dp = mesh.shape["dp"]
    tensor = mesh.shape["tensor"]
    devices = np.asarray(mesh.devices).reshape(dp // 4, 2, 2, tensor)
    fine = Mesh(devices, TOKS)
    rows = P(TOKS, None)
    return jax.shard_map(
        local,
        mesh=fine,
        in_specs=(
            P(("q", "x", "c"), "tensor"),
            P("tensor", None),
            rows,
            P(),
            P(),
            P(),
            rows,
            rows,
            rows,
            P(),
            P(),
            P(TOKS),
            P(),
        ),
        out_specs=(rows, P(), P()),
        check_vma=False,
    )
```

```python
import jax
import jax.numpy as jnp
import numpy as np
from jax import lax
from jax.sharding import Mesh
from jax.sharding import PartitionSpec as P

SEQ = 512


label_weight = 0.5
teacher_eps = 1e-05
student_eps = 1e-07

TOKS = ("q", "x", "c", "tensor")
GROUP = ("x", "c", "tensor")


def norm_rows(values, gain_vec, epsilon):
    center = values - jnp.mean(values, axis=-1, keepdims=True)
    spread = jnp.mean(center * center, axis=-1, keepdims=True)
    inverse = lax.rsqrt(spread + epsilon)
    scaled = center * inverse
    return (scaled * gain_vec, scaled, inverse)


def folder(ordered, row_piece):
    return jnp.dot(ordered, row_piece, preferred_element_type=jnp.float32)


def teacher_attention(context, w_out, tok_rows, ride):
    tensor_size = lax.axis_size("tensor")
    partial = jnp.dot(context, w_out, preferred_element_type=jnp.float32).astype(jnp.bfloat16)
    partial, ride = lax.optimization_barrier((partial, ride))
    if tensor_size != 2:
        return lax.psum_scatter(
            partial, "tensor", scatter_dimension=0, tiled=True
        ).astype(jnp.float32), ride
    me = lax.axis_index("tensor")
    halves = partial.reshape(2, tok_rows, partial.shape[1])
    mine = jnp.where(me == 0, halves[0], halves[1])
    theirs = jnp.where(me == 0, halves[1], halves[0])
    got = lax.ppermute(theirs, "tensor", perm=[(0, 1), (1, 0)])
    return mine.astype(jnp.float32) + got.astype(jnp.float32), ride


def butterfly_sum(value, axes):
    for axis in axes:
        size = lax.axis_size(axis)
        if size & (size - 1):
            value = lax.psum(value, axis)
            continue
        step = 1
        while step < size:
            value = value + lax.ppermute(
                value, axis, perm=[(i, i ^ step) for i in range(size)]
            )
            step *= 2
    return value


def group_gather(value):
    chips = ("x", "tensor")
    n = lax.axis_size(chips)
    parts = [value] + [
        lax.ppermute(value, chips, perm=[(i, (i - k) % n) for i in range(n)])
        for k in range(1, n)
    ]
    plane = jnp.concatenate(parts, axis=0)
    other = lax.ppermute(plane, "c", perm=[(0, 1), (1, 0)])
    return jnp.concatenate([plane, other], axis=0)


def group_order():
    chips = ("x", "tensor")
    n = lax.axis_size(chips)
    tensor = lax.axis_size("tensor")
    core = lax.axis_index("c")
    chip = (lax.axis_index(chips) + jnp.arange(n, dtype=jnp.int32)) % n
    x, t = chip // tensor, chip % tensor
    return jnp.concatenate([(x * 2 + core) * tensor + t, (x * 2 + 1 - core) * tensor + t])


def local(
    context,
    w_out,
    teacher_input,
    teacher_gain,
    layer_weights,
    teacher_head,
    student_hidden,
    student_input,
    down_weight,
    student_gain,
    student_head,
    labels,
    lengths,
):
    tok_rows = teacher_input.shape[0]
    group = lax.axis_size(GROUP)
    outer = lax.axis_size("q")
    hidden_cols = student_hidden.shape[1]
    block = hidden_cols // (group * outer)
    hidden_split = student_hidden.reshape(tok_rows, outer, group, block)
    hidden_split = jnp.transpose(hidden_split, (2, 0, 1, 3)).reshape(group, tok_rows, outer * block)
    attention, hidden_split = teacher_attention(context, w_out, tok_rows, hidden_split)
    me = lax.axis_index(GROUP)
    pieces = [hidden_split[me]]
    for k in range(1, group):
        send = lax.dynamic_index_in_dim(hidden_split, (me - k) % group, 0, keepdims=False)
        pieces.append(
            lax.ppermute(send, GROUP, perm=[(i, (i - k) % group) for i in range(group)])
        )
    hidden_mine = jnp.take(jnp.roll(jnp.stack(pieces), me, axis=0), group_order(), axis=0)
    hidden_mine = hidden_mine.reshape(group * tok_rows, -1)
    hidden_mine, attention = lax.optimization_barrier((hidden_mine, attention))
    residual = teacher_input.astype(jnp.float32)
    layer_out = norm_rows(residual + attention, teacher_gain.astype(jnp.float32), teacher_eps)[0]
    blended = (layer_weights[0] * residual + layer_weights[1] * layer_out).astype(jnp.bfloat16)
    teacher_logits = jnp.dot(blended, teacher_head, preferred_element_type=jnp.float32)
    teacher_logp = jax.nn.log_softmax(teacher_logits, axis=-1)
    teacher_prob = jnp.exp(teacher_logp)
    ffn_out = folder(student_hidden, lax.all_gather(down_weight, TOKS, axis=0, tiled=True))
    student_scale = student_gain.astype(jnp.float32)
    normed, scaled, inverse = norm_rows(
        student_input.astype(jnp.float32) + ffn_out, student_scale, student_eps
    )
    features = normed.astype(jnp.bfloat16)
    student_logits = jnp.dot(features, student_head, preferred_element_type=jnp.float32)
    student_logp = jax.nn.log_softmax(student_logits, axis=-1)
    student_prob = jnp.exp(student_logp)
    first_token = lax.axis_index(TOKS) * tok_rows
    positions = first_token + jnp.arange(tok_rows, dtype=jnp.int32)
    sentence = positions // SEQ
    matches = sentence[:, None] == jnp.arange(lengths.shape[0], dtype=jnp.int32)[None, :]
    lengths_tok = jnp.sum(jnp.where(matches, lengths[None, :], 0), axis=1)
    validity = (positions % SEQ < lengths_tok).astype(jnp.float32)
    onehot = (
        labels[:, None] == jnp.arange(teacher_logits.shape[1], dtype=jnp.int32)[None, :]
    ).astype(jnp.float32)
    token_loss = jnp.sum(
        teacher_prob * (teacher_logp - student_logp), axis=1
    ) - label_weight * jnp.sum(onehot * student_logp, axis=1)
    loss_part = jnp.sum(validity * token_loss)
    logit_grad = (
        validity[:, None]
        * ((1.0 + label_weight) * student_prob - teacher_prob - label_weight * onehot)
    ).astype(jnp.bfloat16)
    head_term = lax.dot_general(
        features, logit_grad, (((0,), (0,)), ((), ())), preferred_element_type=jnp.float32
    )
    norm_grad = (
        jnp.dot(logit_grad, student_head.T, preferred_element_type=jnp.float32) * student_scale
    )
    grad_out = (
        (
            norm_grad
            - jnp.mean(norm_grad, axis=-1, keepdims=True)
            - scaled * jnp.mean(norm_grad * scaled, axis=-1, keepdims=True)
        )
        * inverse
    ).astype(jnp.bfloat16)
    grad_out_group = group_gather(grad_out)
    grad_block = lax.dot_general(
        hidden_mine, grad_out_group, (((0,), (0,)), ((), ())), preferred_element_type=jnp.float32
    )
    grad_down = lax.psum_scatter(
        grad_block, "q", scatter_dimension=0, tiled=True
    )
    classes = head_term.shape[1]
    packed = jnp.concatenate(
        [head_term.reshape(-1), jnp.stack([loss_part, jnp.sum(validity)])]
    )
    packed = butterfly_sum(packed, ("tensor", "c", "x", "q"))
    head_total = packed[: head_term.size].reshape(-1, classes)
    return (grad_down, head_total, packed[head_term.size] / packed[head_term.size + 1])


def solution(mesh):
    dp = mesh.shape["dp"]
    tensor = mesh.shape["tensor"]
    devices = np.asarray(mesh.devices).reshape(dp // 4, 2, 2, tensor)
    fine = Mesh(devices, TOKS)
    rows = P(TOKS, None)
    return jax.shard_map(
        local,
        mesh=fine,
        in_specs=(
            P(("q", "x", "c"), "tensor"),
            P("tensor", None),
            rows,
            P(),
            P(),
            P(),
            rows,
            rows,
            rows,
            P(),
            P(),
            P(TOKS),
            P(),
        ),
        out_specs=(rows, P(), P()),
        check_vma=False,
    )
```

```python
import jax
import jax.numpy as jnp
import numpy as np
from jax import lax
from jax.sharding import Mesh
from jax.sharding import PartitionSpec as P

SEQ = 512


label_weight = 0.5
teacher_eps = 1e-05
student_eps = 1e-07

TOKS = ("q", "x", "c", "tensor")
GROUP = ("x", "c", "tensor")


def norm_rows(values, gain_vec, epsilon):
    center = values - jnp.mean(values, axis=-1, keepdims=True)
    spread = jnp.mean(center * center, axis=-1, keepdims=True)
    inverse = lax.rsqrt(spread + epsilon)
    scaled = center * inverse
    return (scaled * gain_vec, scaled, inverse)


def folder(ordered, row_piece):
    return jnp.dot(ordered, row_piece, preferred_element_type=jnp.float32)


def teacher_attention(context, w_out, tok_rows, ride):
    tensor_size = lax.axis_size("tensor")
    partial = jnp.dot(context, w_out, preferred_element_type=jnp.float32).astype(jnp.bfloat16)
    if tensor_size != 2:
        return lax.optimization_barrier((lax.psum_scatter(
            partial, "tensor", scatter_dimension=0, tiled=True
        ).astype(jnp.float32), ride))
    me = lax.axis_index("tensor")
    halves = partial.reshape(2, tok_rows, partial.shape[1])
    mine = jnp.where(me == 0, halves[0], halves[1])
    theirs = jnp.where(me == 0, halves[1], halves[0])
    got = lax.ppermute(theirs, "tensor", perm=[(0, 1), (1, 0)])
    return lax.optimization_barrier((mine.astype(jnp.float32) + got.astype(jnp.float32), ride))


def butterfly_sum(value, axes):
    for axis in axes:
        size = lax.axis_size(axis)
        if size & (size - 1):
            value = lax.psum(value, axis)
            continue
        step = 1
        while step < size:
            value = value + lax.ppermute(
                value, axis, perm=[(i, i ^ step) for i in range(size)]
            )
            step *= 2
    return value


def group_gather(value):
    chips = ("x", "tensor")
    n = lax.axis_size(chips)
    parts = [value] + [
        lax.ppermute(value, chips, perm=[(i, (i - k) % n) for i in range(n)])
        for k in range(1, n)
    ]
    plane = jnp.concatenate(parts, axis=0)
    other = lax.ppermute(plane, "c", perm=[(0, 1), (1, 0)])
    return jnp.concatenate([plane, other], axis=0)


def group_order():
    chips = ("x", "tensor")
    n = lax.axis_size(chips)
    tensor = lax.axis_size("tensor")
    core = lax.axis_index("c")
    chip = (lax.axis_index(chips) + jnp.arange(n, dtype=jnp.int32)) % n
    x, t = chip // tensor, chip % tensor
    return jnp.concatenate([(x * 2 + core) * tensor + t, (x * 2 + 1 - core) * tensor + t])


def local(
    context,
    w_out,
    teacher_input,
    teacher_gain,
    layer_weights,
    teacher_head,
    student_hidden,
    student_input,
    down_weight,
    student_gain,
    student_head,
    labels,
    lengths,
):
    tok_rows = teacher_input.shape[0]
    group = lax.axis_size(GROUP)
    outer = lax.axis_size("q")
    hidden_cols = student_hidden.shape[1]
    block = hidden_cols // (group * outer)
    hidden_split = student_hidden.reshape(tok_rows, outer, group, block)
    hidden_split = jnp.transpose(hidden_split, (2, 0, 1, 3)).reshape(group, tok_rows, outer * block)
    attention, hidden_split = teacher_attention(context, w_out, tok_rows, hidden_split)
    me = lax.axis_index(GROUP)
    pieces = [hidden_split[me]]
    for k in range(1, group):
        send = lax.dynamic_index_in_dim(hidden_split, (me - k) % group, 0, keepdims=False)
        pieces.append(
            lax.ppermute(send, GROUP, perm=[(i, (i - k) % group) for i in range(group)])
        )
    hidden_mine = jnp.take(jnp.roll(jnp.stack(pieces), me, axis=0), group_order(), axis=0)
    hidden_mine = hidden_mine.reshape(group * tok_rows, -1)
    hidden_mine, attention = lax.optimization_barrier((hidden_mine, attention))
    residual = teacher_input.astype(jnp.float32)
    layer_out = norm_rows(residual + attention, teacher_gain.astype(jnp.float32), teacher_eps)[0]
    blended = (layer_weights[0] * residual + layer_weights[1] * layer_out).astype(jnp.bfloat16)
    teacher_logits = jnp.dot(blended, teacher_head, preferred_element_type=jnp.float32)
    teacher_logp = jax.nn.log_softmax(teacher_logits, axis=-1)
    teacher_prob = jnp.exp(teacher_logp)
    ffn_out = folder(student_hidden, lax.all_gather(down_weight, TOKS, axis=0, tiled=True))
    student_scale = student_gain.astype(jnp.float32)
    normed, scaled, inverse = norm_rows(
        student_input.astype(jnp.float32) + ffn_out, student_scale, student_eps
    )
    features = normed.astype(jnp.bfloat16)
    student_logits = jnp.dot(features, student_head, preferred_element_type=jnp.float32)
    student_logp = jax.nn.log_softmax(student_logits, axis=-1)
    student_prob = jnp.exp(student_logp)
    first_token = lax.axis_index(TOKS) * tok_rows
    positions = first_token + jnp.arange(tok_rows, dtype=jnp.int32)
    sentence = positions // SEQ
    matches = sentence[:, None] == jnp.arange(lengths.shape[0], dtype=jnp.int32)[None, :]
    lengths_tok = jnp.sum(jnp.where(matches, lengths[None, :], 0), axis=1)
    validity = (positions % SEQ < lengths_tok).astype(jnp.float32)
    onehot = (
        labels[:, None] == jnp.arange(teacher_logits.shape[1], dtype=jnp.int32)[None, :]
    ).astype(jnp.float32)
    token_loss = jnp.sum(
        teacher_prob * (teacher_logp - student_logp), axis=1
    ) - label_weight * jnp.sum(onehot * student_logp, axis=1)
    loss_part = jnp.sum(validity * token_loss)
    logit_grad = (
        validity[:, None]
        * ((1.0 + label_weight) * student_prob - teacher_prob - label_weight * onehot)
    ).astype(jnp.bfloat16)
    head_term = lax.dot_general(
        features, logit_grad, (((0,), (0,)), ((), ())), preferred_element_type=jnp.float32
    )
    norm_grad = (
        jnp.dot(logit_grad, student_head.T, preferred_element_type=jnp.float32) * student_scale
    )
    grad_out = (
        (
            norm_grad
            - jnp.mean(norm_grad, axis=-1, keepdims=True)
            - scaled * jnp.mean(norm_grad * scaled, axis=-1, keepdims=True)
        )
        * inverse
    ).astype(jnp.bfloat16)
    grad_out_group = group_gather(grad_out)
    grad_block = lax.dot_general(
        hidden_mine, grad_out_group, (((0,), (0,)), ((), ())), preferred_element_type=jnp.float32
    )
    grad_down = lax.psum_scatter(
        grad_block, "q", scatter_dimension=0, tiled=True
    )
    classes = head_term.shape[1]
    packed = jnp.concatenate(
        [head_term.reshape(-1), jnp.stack([loss_part, jnp.sum(validity)])]
    )
    packed = butterfly_sum(packed, ("tensor", "c", "x", "q"))
    head_total = packed[: head_term.size].reshape(-1, classes)
    return (grad_down, head_total, packed[head_term.size] / packed[head_term.size + 1])


def solution(mesh):
    dp = mesh.shape["dp"]
    tensor = mesh.shape["tensor"]
    devices = np.asarray(mesh.devices).reshape(dp // 4, 2, 2, tensor)
    fine = Mesh(devices, TOKS)
    rows = P(TOKS, None)
    return jax.shard_map(
        local,
        mesh=fine,
        in_specs=(
            P(("q", "x", "c"), "tensor"),
            P("tensor", None),
            rows,
            P(),
            P(),
            P(),
            rows,
            rows,
            rows,
            P(),
            P(),
            P(TOKS),
            P(),
        ),
        out_specs=(rows, P(), P()),
        check_vma=False,
    )
```
